256 devices in a mesh: expert: 16 (over y, x_hi, core), dp: 16 (over x_lo, z).
Axes of the slice: x: 4 (x_hi: 2, x_lo: 2; x = x_hi * 2 + x_lo), y: 4, z: 8, core: 2. Of those that a mesh axis runs over, the one named last changes fastest.
Arguments:
- tokens: bfloat16 [32768, 2048], P(('expert', 'dp')), may hold values from -6 to 6
- cotangent: bfloat16 [32768, 2048], P(('expert', 'dp')), may hold values from -6 to 6
- expert_ids: int32 [32768, 8], P(('expert', 'dp')), may hold values from 0 to 127, as said below
- gate_weights: float32 [32768, 8], P(('expert', 'dp')), may hold values from 0.05 to 1
- placement: int32 [16], replicated, may hold values from 0 to 15, as said below
- w_in: bfloat16 [16, 2048, 1536], P('expert'), may hold values from -0.125 to 0.125
- w_out: bfloat16 [16, 768, 2048], P('expert'), may hold values from -0.21875 to 0.21875
Outputs:
- mixed: bfloat16 [32768, 2048], P(('expert', 'dp'))
- x_grad: bfloat16 [32768, 2048], P(('expert', 'dp'))
- gate_grad: float32 [32768, 8], P(('expert', 'dp'))
- w_in_grad: bfloat16 [16, 2048, 1536], P('expert', 'dp')
- w_out_grad: bfloat16 [16, 768, 2048], P('expert', 'dp')
The draws below stay inside these ranges and needn't reach their ends.
Inputs may be any that keep to these rules, and one draw needn't show every extreme that they name: `expert_ids`: each row names 8 different experts, at most two of them below 16. Among the 128 tokens of one device (an aligned block of rows, one data group every 16 blocks), no expert below 16 is named by more than 16 tokens, and in every data group one such expert is named by exactly 16 tokens of every device of the group. placement[i] is i or (i + 8) % 16, and placement[placement[i]] = i; at least one pair exchanges and at least one pair stays.
All inputs are finite; a program needn't handle non-finite values.
Results may differ from the reference program's by a relative error of at most 0.018.
Values may be sent and summed in bfloat16 or wider, within the bound.
No kernel may reach another device: no remote copies, remote signals or barrier semaphores. Data moves between devices by JAX's collectives and lax.ppermute only.
A program may use at most 128 MiB of HBM per device.

```python
import math
import jax
import jax.numpy as jnp
from jax import lax

D = 2048
FF = 768
TOP = 8
TOK_DEV = 128
CAP = 16
EXPERTS = 16
ROUTED = 128
GROUPS = 16
TOKENS = 32768


def draw_expert_ids(key, part):
    blocks = TOKENS // TOK_DEV
    group_count = blocks // EXPERTS
    key_level, key_full, key_count, key_order, key_offset, key_turn = jax.random.split(key, 6)
    level = jax.random.randint(key_level, (group_count, EXPERTS), CAP // 2, CAP + 1)
    full_expert = jax.random.randint(key_full, (group_count,), 0, EXPERTS)
    block_group = jnp.arange(blocks, dtype=jnp.int32) % group_count
    raw_count = jax.random.randint(key_count, (blocks, EXPERTS), 0, 1 << 20)
    block_level = level[block_group]
    counts = block_level - raw_count % (block_level // 2 + 1)
    expert_lane = jnp.arange(EXPERTS, dtype=jnp.int32)
    counts = jnp.where(expert_lane[None, :] == full_expert[block_group][:, None], CAP, counts)
    starts = jnp.cumsum(counts, axis=1) - counts
    order_keys = jax.random.split(key_order, blocks)
    order = jax.vmap(lambda subkey: jax.random.permutation(subkey, TOK_DEV))(order_keys).astype(jnp.int32)
    covered = (order[:, :, None] - starts[:, None, :]) % TOK_DEV < counts[:, None, :]
    covered = covered.reshape(TOKENS, EXPERTS)
    cover_count = jnp.sum(covered.astype(jnp.int32), axis=1)
    first_pick = jnp.argmax(covered, axis=1).astype(jnp.int32)
    last_pick = (EXPERTS - 1 - jnp.argmax(covered[:, ::-1], axis=1)).astype(jnp.int32)
    offset = jax.random.randint(key_offset, (TOKENS,), 0, ROUTED - EXPERTS)
    turn = jax.random.randint(key_turn, (TOKENS,), 0, TOP)
    slot_lane = jnp.arange(TOP, dtype=jnp.int32)
    outside = EXPERTS + (offset[:, None] + slot_lane[None, :]) % (ROUTED - EXPERTS)
    listed = jnp.where((slot_lane[None, :] == 0) & (cover_count[:, None] >= 1), first_pick[:, None], outside)
    listed = jnp.where((slot_lane[None, :] == 1) & (cover_count[:, None] >= 2), last_pick[:, None], listed)
    rolled = ((slot_lane[None, :] + turn[:, None]) % TOP).astype(jnp.int32)
    return jnp.take_along_axis(listed, rolled, axis=1).astype(jnp.int32)


def draw_placement(key, part):
    half_count = EXPERTS // 2
    key_flag, key_first, key_second = jax.random.split(key, 3)
    flags = jax.random.randint(key_flag, (half_count,), 0, 2)
    first_pair = jax.random.randint(key_first, (), 0, half_count)
    second_pair = (first_pair + jax.random.randint(key_second, (), 1, half_count)) % half_count
    pair_lane = jnp.arange(half_count, dtype=jnp.int32)
    flags = jnp.where(pair_lane == first_pair, 1, jnp.where(pair_lane == second_pair, 0, flags))
    return jnp.concatenate([pair_lane + half_count * flags, pair_lane + half_count * (1 - flags)]).astype(jnp.int32)


def levels(stream_key, dims, cuts, low, high):
    factor_of, own = 1.0, jax.random.fold_in(stream_key, 6)
    for dim, parts in cuts:
        draws = jnp.exp(jax.random.uniform(jax.random.fold_in(own, dim), (parts,), jnp.float32, low / len(cuts), high / len(cuts)))
        factor_of = factor_of * jnp.repeat(draws, dims[dim] // parts).reshape([-1 if axis == dim else 1 for axis in range(len(dims))])
    return factor_of


def bell_draw(key, dims, spread, limit, pieces=(), held_as=jnp.bfloat16):
    level = levels(key, dims, pieces, -0.22, 0.18) if pieces else 1.0
    result = jax.random.normal(key, dims, jnp.float32) * spread * level
    return jnp.minimum(jnp.maximum(result, -limit), limit).astype(held_as)


def setup_inputs(seed: int = 0) -> dict:
    splits = jax.random.split(jax.random.key(seed), 8)
    tokens = bell_draw(splits[0], (TOKENS, D), 1.0, 6.0, ((0, 256),))
    cotangent = bell_draw(splits[1], (TOKENS, D), 1.0, 6.0, ((0, 256),))
    expert_ids = draw_expert_ids(jax.random.fold_in(splits[7], 71), 0)
    gate_weights = jnp.clip(jnp.exp(math.log(1.0) - 2.9957323 * jax.random.uniform(splits[3], (TOKENS, TOP), jnp.float32) ** levels(splits[3], (TOKENS, TOP), ((0, 256),), -0.2, 0.2)), 0.05, 1.0)
    placement = draw_placement(jax.random.fold_in(splits[7], 71), 0)
    w_in = bell_draw(splits[5], (EXPERTS, D, 2 * FF), D ** -0.5, 0.125, ((0, 16),))
    w_out = bell_draw(splits[6], (EXPERTS, FF, D), FF ** -0.5, 0.21875, ((0, 16),))
    return {"tokens": tokens, "cotangent": cotangent, "expert_ids": expert_ids, "gate_weights": gate_weights, "placement": placement, "w_in": w_in, "w_out": w_out}


def reference(tokens, cotangent, expert_ids, gate_weights, placement, w_in, w_out):
    highest = lax.Precision.HIGHEST
    position = jnp.arange(TOKENS, dtype=jnp.int32)
    group_of = (position // TOK_DEV) % GROUPS
    group_lane = jnp.arange(GROUPS, dtype=jnp.int32)
    row_limit = EXPERTS * CAP

    def one_expert(carry, expert):
        mixed_sum, grad_sum, gate_sum = carry
        is_hit = expert_ids == expert
        chosen = jnp.any(is_hit, axis=1)
        gate_value = jnp.sum(jnp.where(is_hit, gate_weights, 0.0), axis=1)
        sort_keys = jnp.where(chosen[None, :] & (group_of[None, :] == group_lane[:, None]), position[None, :], TOKENS)
        sort_keys = jnp.sort(sort_keys, axis=1)[:, :row_limit].astype(jnp.int32)
        is_valid = sort_keys < TOKENS
        row_index = jnp.minimum(sort_keys, TOKENS - 1).astype(jnp.int32)
        picked_x = jnp.where(is_valid[..., None], tokens[row_index], jnp.zeros((), tokens.dtype))
        weight_in = lax.dynamic_index_in_dim(w_in, expert, 0, keepdims=False).astype(jnp.float32)
        weight_out = lax.dynamic_index_in_dim(w_out, expert, 0, keepdims=False).astype(jnp.float32)
        pre = jnp.einsum("gmd,df->gmf", picked_x.astype(jnp.float32), weight_in, precision=highest)
        gate_pre = pre[..., :FF]
        up_pre = pre[..., FF:]
        sigmoid_gate = jax.nn.sigmoid(gate_pre)
        activated = gate_pre * sigmoid_gate
        hidden = (activated * up_pre).astype(jnp.bfloat16)
        expert_out = jnp.einsum("gmf,fd->gmd", hidden.astype(jnp.float32), weight_out, precision=highest).astype(jnp.bfloat16)
        pick_gate = jnp.where(is_valid, gate_value[row_index], 0.0)
        picked_dy = cotangent[row_index].astype(jnp.float32)
        scaled = (picked_dy * pick_gate[..., None]).astype(jnp.bfloat16)
        hidden_grad = jnp.einsum("gmd,fd->gmf", scaled.astype(jnp.float32), weight_out, precision=highest)
        gate_up_grad = jnp.concatenate(
            [hidden_grad * up_pre * sigmoid_gate * (1.0 + gate_pre * (1.0 - sigmoid_gate)), hidden_grad * activated],
            axis=-1).astype(jnp.bfloat16)
        pick_grad = jnp.einsum("gmf,df->gmd", gate_up_grad.astype(jnp.float32), weight_in, precision=highest).astype(jnp.bfloat16)
        partial_in = jnp.einsum("gmd,gmf->gdf", picked_x.astype(jnp.float32), gate_up_grad.astype(jnp.float32), precision=highest).astype(jnp.bfloat16)
        partial_out = jnp.einsum("gmf,gmd->gfd", hidden.astype(jnp.float32), scaled.astype(jnp.float32), precision=highest).astype(jnp.bfloat16)
        grad_in = (jnp.sum(partial_in.astype(jnp.float32), axis=0) / GROUPS).astype(jnp.bfloat16)
        grad_out = (jnp.sum(partial_out.astype(jnp.float32), axis=0) / GROUPS).astype(jnp.bfloat16)
        flat_index = row_index.reshape(-1)
        flat_valid = is_valid.reshape(-1)
        contribution = (pick_gate[..., None] * expert_out.astype(jnp.float32)).reshape(-1, D)
        mixed_sum = mixed_sum.at[flat_index].add(jnp.where(flat_valid[:, None], contribution, 0.0))
        grad_sum = grad_sum.at[flat_index].add(jnp.where(flat_valid[:, None], pick_grad.astype(jnp.float32).reshape(-1, D), 0.0))
        score = jnp.sum(picked_dy * expert_out.astype(jnp.float32), axis=-1).reshape(-1)
        token_score = jnp.zeros((TOKENS,), jnp.float32).at[flat_index].add(jnp.where(flat_valid, score, 0.0))
        gate_sum = gate_sum + jnp.where(is_hit, token_score[:, None], 0.0)
        return (mixed_sum, grad_sum, gate_sum), (grad_in, grad_out)

    start = (jnp.zeros((TOKENS, D), jnp.float32), jnp.zeros((TOKENS, D), jnp.float32), jnp.zeros((TOKENS, TOP), jnp.float32))
    final, stacked = lax.scan(one_expert, start, jnp.arange(EXPERTS, dtype=jnp.int32))
    mixed_sum, grad_sum, gate_sum = final
    grads_in, grads_out = stacked
    return (mixed_sum.astype(jnp.bfloat16), grad_sum.astype(jnp.bfloat16), gate_sum,
            jnp.take(grads_in, placement, axis=0), jnp.take(grads_out, placement, axis=0))
```

```python
import jax
import jax.numpy as jnp
from jax import lax
from jax.sharding import PartitionSpec as P


def partner_2(block, axis, apart):
    count = lax.axis_size(axis)
    route = []
    for low in range(count):
        high = low | 1 << apart
        if high != low and high < count:
            route += [(low, high), (high, low)]
    return lax.ppermute(block, axis, route)


def shards(tokens, cotangent, expert_ids, gate_weights, placement, w_in, w_out):
    expert_count = lax.axis_size("expert")
    group_count = lax.axis_size("dp")
    own_index = lax.axis_index("expert")
    tok_rows = tokens.shape[0]
    model_width = tokens.shape[1]
    hidden_units = w_out.shape[1]
    pick_count = expert_ids.shape[1]
    capacity = tok_rows // 8
    slot_count = expert_count * capacity
    half_bit = expert_count.bit_length() - 2
    expert_lane = jnp.arange(expert_count, dtype=jnp.int32)
    partner = jnp.sum(jnp.where(expert_lane == own_index, placement, 0))
    is_moved = partner != own_index
    weight_in = w_in[0]
    weight_out = w_out[0]
    device_hot = (expert_ids.reshape(-1)[:, None] == expert_lane[None, :]).astype(jnp.int32)
    slot_rank = jnp.cumsum(device_hot, axis=0) - device_hot
    slot_place = jnp.sum((slot_rank + expert_lane[None, :] * capacity) * device_hot, axis=1)
    is_live = jnp.sum(device_hot, axis=1) > 0
    slot_place = jnp.where(is_live, slot_place, -1).reshape(tok_rows, pick_count)
    slot_hot = slot_place[:, :, None] == jnp.arange(slot_count, dtype=jnp.int32)[None, None, :]
    select = jnp.sum(slot_hot.astype(jnp.bfloat16), axis=1)
    weigh = jnp.sum(jnp.where(slot_hot, gate_weights[:, :, None], 0.0), axis=1)
    slot_gate = jnp.sum(weigh, axis=0)
    send_x = jnp.einsum("ts,td->sd", select, tokens, preferred_element_type=jnp.float32).astype(
        jnp.bfloat16
    )
    send_dy = jnp.einsum("ts,td->sd", select, cotangent, preferred_element_type=jnp.float32)
    send_c = (send_dy * slot_gate[:, None]).astype(jnp.bfloat16)
    send_x = send_x.reshape(expert_count, capacity, model_width)
    send_c = send_c.reshape(expert_count, capacity, model_width)
    arrived_x = lax.all_to_all(send_x, "expert", split_axis=0, concat_axis=0, tiled=True)
    rows_x = arrived_x.reshape(slot_count, model_width)
    pre = jnp.dot(rows_x, weight_in, preferred_element_type=jnp.float32)
    gate_pre = pre[:, :hidden_units]
    up_pre = pre[:, hidden_units:]
    sigmoid_gate = jax.nn.sigmoid(gate_pre)
    activated = gate_pre * sigmoid_gate
    hidden = (activated * up_pre).astype(jnp.bfloat16)
    expert_out = jnp.dot(hidden, weight_out, preferred_element_type=jnp.float32).astype(
        jnp.bfloat16
    )
    returned = lax.all_to_all(
        expert_out.reshape(expert_count, capacity, model_width),
        "expert",
        split_axis=0,
        concat_axis=0,
        tiled=True,
    )
    returned = returned.reshape(slot_count, model_width)
    mixed = jnp.dot(
        weigh,
        returned.astype(jnp.float32),
        precision=lax.Precision.HIGHEST,
        preferred_element_type=jnp.float32,
    ).astype(jnp.bfloat16)
    scores = jnp.einsum("td,sd->ts", cotangent, returned, preferred_element_type=jnp.float32)
    gate_grad = jnp.sum(jnp.where(slot_hot, scores[:, None, :], 0.0), axis=2)
    arrived_c = lax.all_to_all(send_c, "expert", split_axis=0, concat_axis=0, tiled=True)
    rows_c = arrived_c.reshape(slot_count, model_width)
    hidden_grad = jnp.einsum("sd,fd->sf", rows_c, weight_out, preferred_element_type=jnp.float32)
    slope = sigmoid_gate * (1.0 + gate_pre * (1.0 - sigmoid_gate))
    gate_up_grad = jnp.concatenate(
        [hidden_grad * up_pre * slope, hidden_grad * activated], axis=1
    ).astype(jnp.bfloat16)
    pick_grad = jnp.einsum(
        "sf,df->sd", gate_up_grad, weight_in, preferred_element_type=jnp.float32
    ).astype(jnp.bfloat16)
    back = lax.all_to_all(
        pick_grad.reshape(expert_count, capacity, model_width),
        "expert",
        split_axis=0,
        concat_axis=0,
        tiled=True,
    )
    back = back.reshape(slot_count, model_width)
    x_grad = jnp.einsum("ts,sd->td", select, back, preferred_element_type=jnp.float32).astype(
        jnp.bfloat16
    )
    grad_in = (
        lax.psum_scatter(
            jnp.einsum(
                "sd,sf->df", rows_x, gate_up_grad, preferred_element_type=jnp.float32
            ).astype(jnp.bfloat16),
            "dp",
            scatter_dimension=0,
            tiled=True,
        ).astype(jnp.float32)
        / group_count
    ).astype(jnp.bfloat16)
    grad_out = (
        lax.psum_scatter(
            jnp.einsum("sf,sd->fd", hidden, rows_c, preferred_element_type=jnp.float32).astype(
                jnp.bfloat16
            ),
            "dp",
            scatter_dimension=0,
            tiled=True,
        ).astype(jnp.float32)
        / group_count
    ).astype(jnp.bfloat16)
    swapped = partner_2((grad_in, grad_out), "expert", half_bit)
    grad_in = jnp.where(is_moved, swapped[0], grad_in)
    grad_out = jnp.where(is_moved, swapped[1], grad_out)
    return (mixed, x_grad, gate_grad, grad_in[None], grad_out[None])


def solution(mesh):
    placed = (
        P(("expert", "dp"), None),
        P(("expert", "dp"), None),
        P(("expert", "dp"), None),
        P(("expert", "dp"), None),
        P(),
        P("expert", None, None),
        P("expert", None, None),
    )
    return jax.shard_map(
        shards,
        mesh=mesh,
        in_specs=placed,
        out_specs=(
            P(("expert", "dp"), None),
            P(("expert", "dp"), None),
            P(("expert", "dp"), None),
            P("expert", "dp", None),
            P("expert", "dp", None),
        ),
        check_vma=False,
    )
```

```python
import jax
import jax.numpy as jnp
from jax import lax
from jax.sharding import PartitionSpec as P


def partner_2(block, axis, apart):
    count = lax.axis_size(axis)
    route = []
    for low in range(count):
        high = low | 1 << apart
        if high != low and high < count:
            route += [(low, high), (high, low)]
    return lax.ppermute(block, axis, route)


def exchange(block, expert_count, capacity):
    shaped = block.reshape(expert_count, capacity, block.shape[-1])
    arrived = lax.all_to_all(shaped, "expert", split_axis=0, concat_axis=0, tiled=True)
    return arrived.reshape(expert_count * capacity, block.shape[-1])


def shards(tokens, cotangent, expert_ids, gate_weights, placement, w_in, w_out):
    expert_count = lax.axis_size("expert")
    group_count = lax.axis_size("dp")
    own_index = lax.axis_index("expert")
    tok_rows = tokens.shape[0]
    model_width = tokens.shape[1]
    hidden_units = w_out.shape[1]
    pick_count = expert_ids.shape[1]
    capacity = tok_rows // 8
    slot_count = expert_count * capacity
    pick_rows = tok_rows * pick_count
    half_bit = expert_count.bit_length() - 2
    expert_lane = jnp.arange(expert_count, dtype=jnp.int32)
    partner = jnp.sum(jnp.where(expert_lane == own_index, placement, 0))
    is_moved = partner != own_index
    weight_in = w_in[0]
    weight_out = w_out[0]

    device_hot = (expert_ids.reshape(-1)[:, None] == expert_lane[None, :]).astype(jnp.bfloat16)
    row_lane = jnp.arange(pick_rows, dtype=jnp.int32)
    earlier = (row_lane[None, :] < row_lane[:, None]).astype(jnp.bfloat16)
    slot_rank = jnp.dot(earlier, device_hot, preferred_element_type=jnp.float32).astype(jnp.int32)
    hot = device_hot.astype(jnp.int32)
    slot_place = jnp.sum((slot_rank + expert_lane[None, :] * capacity) * hot, axis=1)
    is_live = jnp.sum(hot, axis=1) > 0
    slot_place = jnp.where(is_live, slot_place, -1).reshape(tok_rows, pick_count)
    slot_hot = slot_place[:, :, None] == jnp.arange(slot_count, dtype=jnp.int32)[None, None, :]
    select = jnp.sum(slot_hot.astype(jnp.bfloat16), axis=1)
    weigh = jnp.sum(jnp.where(slot_hot, gate_weights[:, :, None], 0.0), axis=1)
    slot_gate = jnp.sum(weigh, axis=0)

    send_x = jnp.einsum("ts,td->sd", select, tokens, preferred_element_type=jnp.float32).astype(
        jnp.bfloat16
    )
    send_dy = jnp.einsum("ts,td->sd", select, cotangent, preferred_element_type=jnp.float32)
    send_c = (send_dy * slot_gate[:, None]).astype(jnp.bfloat16)
    arrived = exchange(jnp.concatenate([send_x, send_c], axis=1), expert_count, capacity)
    rows_x = arrived[:, :model_width]
    rows_c = arrived[:, model_width:]

    pre = jnp.dot(rows_x, weight_in, preferred_element_type=jnp.float32)
    gate_pre = pre[:, :hidden_units]
    up_pre = pre[:, hidden_units:]
    sigmoid_gate = jax.nn.sigmoid(gate_pre)
    activated = gate_pre * sigmoid_gate
    hidden = (activated * up_pre).astype(jnp.bfloat16)
    expert_out = jnp.dot(hidden, weight_out, preferred_element_type=jnp.float32).astype(
        jnp.bfloat16
    )

    hidden_grad = jnp.einsum("sd,fd->sf", rows_c, weight_out, preferred_element_type=jnp.float32)
    slope = sigmoid_gate * (1.0 + gate_pre * (1.0 - sigmoid_gate))
    gate_up_grad = jnp.concatenate(
        [hidden_grad * up_pre * slope, hidden_grad * activated], axis=1
    ).astype(jnp.bfloat16)
    part_out = jnp.einsum("sf,sd->fd", hidden, rows_c, preferred_element_type=jnp.float32).astype(
        jnp.bfloat16
    )
    grad_out = lax.psum_scatter(part_out, "dp", scatter_dimension=0, tiled=True)
    part_in = jnp.einsum("sd,sf->df", rows_x, gate_up_grad, preferred_element_type=jnp.float32).astype(
        jnp.bfloat16
    )
    grad_in = lax.psum_scatter(part_in, "dp", scatter_dimension=0, tiled=True)
    pick_grad = jnp.einsum(
        "sf,df->sd", gate_up_grad, weight_in, preferred_element_type=jnp.float32
    ).astype(jnp.bfloat16)

    back = exchange(jnp.concatenate([expert_out, pick_grad], axis=1), expert_count, capacity)
    returned = back[:, :model_width]
    back_grad = back[:, model_width:]
    mixed = jnp.dot(
        weigh,
        returned.astype(jnp.float32),
        precision=lax.Precision.HIGHEST,
        preferred_element_type=jnp.float32,
    ).astype(jnp.bfloat16)
    scores = jnp.einsum("td,sd->ts", cotangent, returned, preferred_element_type=jnp.float32)
    gate_grad = jnp.sum(jnp.where(slot_hot, scores[:, None, :], 0.0), axis=2)
    x_grad = jnp.einsum("ts,sd->td", select, back_grad, preferred_element_type=jnp.float32).astype(
        jnp.bfloat16
    )

    grad_in = (grad_in.astype(jnp.float32) / group_count).astype(jnp.bfloat16)
    grad_out = (grad_out.astype(jnp.float32) / group_count).astype(jnp.bfloat16)
    swapped = partner_2((grad_in, grad_out), "expert", half_bit)
    grad_in = jnp.where(is_moved, swapped[0], grad_in)
    grad_out = jnp.where(is_moved, swapped[1], grad_out)
    return (mixed, x_grad, gate_grad, grad_in[None], grad_out[None])


def solution(mesh):
    placed = (
        P(("expert", "dp"), None),
        P(("expert", "dp"), None),
        P(("expert", "dp"), None),
        P(("expert", "dp"), None),
        P(),
        P("expert", None, None),
        P("expert", None, None),
    )
    return jax.shard_map(
        shards,
        mesh=mesh,
        in_specs=placed,
        out_specs=(
            P(("expert", "dp"), None),
            P(("expert", "dp"), None),
            P(("expert", "dp"), None),
            P("expert", "dp", None),
            P("expert", "dp", None),
        ),
        check_vma=False,
    )
```

```python
import jax
import jax.numpy as jnp
from jax import lax
from jax.sharding import PartitionSpec as P


def partner_2(block, axis, apart):
    count = lax.axis_size(axis)
    route = []
    for low in range(count):
        high = low | 1 << apart
        if high != low and high < count:
            route += [(low, high), (high, low)]
    return lax.ppermute(block, axis, route)


def exchange(block, expert_count, capacity):
    shaped = block.reshape(expert_count, capacity, block.shape[-1])
    arrived = lax.all_to_all(shaped, "expert", split_axis=0, concat_axis=0, tiled=True)
    return arrived.reshape(expert_count * capacity, block.shape[-1])


def shards(tokens, cotangent, expert_ids, gate_weights, placement, w_in, w_out):
    expert_count = lax.axis_size("expert")
    group_count = lax.axis_size("dp")
    own_index = lax.axis_index("expert")
    tok_rows = tokens.shape[0]
    model_width = tokens.shape[1]
    hidden_units = w_out.shape[1]
    pick_count = expert_ids.shape[1]
    capacity = tok_rows // 8
    slot_count = expert_count * capacity
    pick_rows = tok_rows * pick_count
    half_bit = expert_count.bit_length() - 2
    expert_lane = jnp.arange(expert_count, dtype=jnp.int32)
    partner = jnp.sum(jnp.where(expert_lane == own_index, placement, 0))
    is_moved = partner != own_index
    weight_in = w_in[0]
    weight_out = w_out[0]

    device_hot = (expert_ids.reshape(-1)[:, None] == expert_lane[None, :]).astype(jnp.bfloat16)
    row_lane = jnp.arange(pick_rows, dtype=jnp.int32)
    earlier = (row_lane[None, :] < row_lane[:, None]).astype(jnp.bfloat16)
    slot_rank = jnp.dot(earlier, device_hot, preferred_element_type=jnp.float32).astype(jnp.int32)
    hot = device_hot.astype(jnp.int32)
    slot_place = jnp.sum((slot_rank + expert_lane[None, :] * capacity) * hot, axis=1)
    is_live = jnp.sum(hot, axis=1) > 0
    slot_place = jnp.where(is_live, slot_place, -1).reshape(tok_rows, pick_count)
    slot_hot = slot_place[:, :, None] == jnp.arange(slot_count, dtype=jnp.int32)[None, None, :]
    select = jnp.sum(slot_hot.astype(jnp.bfloat16), axis=1)
    weigh = jnp.sum(jnp.where(slot_hot, gate_weights[:, :, None], 0.0), axis=1)
    slot_gate = jnp.sum(weigh, axis=0)

    send_x = jnp.einsum("ts,td->sd", select, tokens, preferred_element_type=jnp.float32).astype(
        jnp.bfloat16
    )
    send_dy = jnp.einsum("ts,td->sd", select, cotangent, preferred_element_type=jnp.float32)
    send_c = (send_dy * slot_gate[:, None]).astype(jnp.bfloat16)
    arrived = exchange(jnp.concatenate([send_x, send_c], axis=1), expert_count, capacity)
    rows_x = arrived[:, :model_width]
    rows_c = arrived[:, model_width:]

    pre = jnp.dot(rows_x, weight_in, preferred_element_type=jnp.float32)
    gate_pre = pre[:, :hidden_units]
    up_pre = pre[:, hidden_units:]
    sigmoid_gate = jax.nn.sigmoid(gate_pre)
    activated = gate_pre * sigmoid_gate
    hidden = (activated * up_pre).astype(jnp.bfloat16)
    expert_out = jnp.dot(hidden, weight_out, preferred_element_type=jnp.float32).astype(
        jnp.bfloat16
    )

    hidden_grad = jnp.einsum("sd,fd->sf", rows_c, weight_out, preferred_element_type=jnp.float32)
    slope = sigmoid_gate * (1.0 + gate_pre * (1.0 - sigmoid_gate))
    gate_up_grad = jnp.concatenate(
        [hidden_grad * up_pre * slope, hidden_grad * activated], axis=1
    ).astype(jnp.bfloat16)
    part_out = jnp.einsum("sf,sd->fd", hidden, rows_c, preferred_element_type=jnp.float32).astype(
        jnp.bfloat16
    )
    part_in = jnp.einsum("sd,sf->df", rows_x, gate_up_grad, preferred_element_type=jnp.float32).astype(
        jnp.bfloat16
    )
    in_rows = model_width // group_count
    in_cols = part_in.shape[1]
    out_rows = hidden_units // group_count
    out_as = out_rows * model_width // in_cols
    joined = jnp.concatenate(
        [
            part_in.reshape(group_count, in_rows, in_cols),
            part_out.reshape(group_count, out_as, in_cols),
        ],
        axis=1,
    ).reshape(group_count * (in_rows + out_as), in_cols)
    reduced = lax.psum_scatter(joined, "dp", scatter_dimension=0, tiled=True)
    pick_grad = jnp.einsum(
        "sf,df->sd", gate_up_grad, weight_in, preferred_element_type=jnp.float32
    ).astype(jnp.bfloat16)

    back = exchange(jnp.concatenate([expert_out, pick_grad], axis=1), expert_count, capacity)
    returned = back[:, :model_width]
    back_grad = back[:, model_width:]
    mixed = jnp.dot(
        weigh,
        returned.astype(jnp.float32),
        precision=lax.Precision.HIGHEST,
        preferred_element_type=jnp.float32,
    ).astype(jnp.bfloat16)
    scores = jnp.einsum("td,sd->ts", cotangent, returned, preferred_element_type=jnp.float32)
    gate_grad = jnp.sum(jnp.where(slot_hot, scores[:, None, :], 0.0), axis=2)
    x_grad = jnp.einsum("ts,sd->td", select, back_grad, preferred_element_type=jnp.float32).astype(
        jnp.bfloat16
    )

    reduced = (reduced.astype(jnp.float32) / group_count).astype(jnp.bfloat16)
    swapped = partner_2(reduced, "expert", half_bit)
    reduced = jnp.where(is_moved, swapped, reduced)
    grad_in = reduced[:in_rows]
    grad_out = reduced[in_rows:].reshape(out_rows, model_width)
    return (mixed, x_grad, gate_grad, grad_in[None], grad_out[None])


def solution(mesh):
    placed = (
        P(("expert", "dp"), None),
        P(("expert", "dp"), None),
        P(("expert", "dp"), None),
        P(("expert", "dp"), None),
        P(),
        P("expert", None, None),
        P("expert", None, None),
    )
    return jax.shard_map(
        shards,
        mesh=mesh,
        in_specs=placed,
        out_specs=(
            P(("expert", "dp"), None),
            P(("expert", "dp"), None),
            P(("expert", "dp"), None),
            P("expert", "dp", None),
            P("expert", "dp", None),
        ),
        check_vma=False,
    )
```

```python
import jax
import jax.numpy as jnp
from jax import lax
from jax.sharding import PartitionSpec as P


def partner_2(block, axis, apart):
    count = lax.axis_size(axis)
    route = []
    for low in range(count):
        high = low | 1 << apart
        if high != low and high < count:
            route += [(low, high), (high, low)]
    return lax.ppermute(block, axis, route)


def exchange(block, expert_count, capacity):
    shaped = block.reshape(expert_count, capacity, block.shape[-1])
    arrived = lax.all_to_all(shaped, "expert", split_axis=0, concat_axis=0, tiled=True)
    return arrived.reshape(expert_count * capacity, block.shape[-1])


def shards(tokens, cotangent, expert_ids, gate_weights, placement, w_in, w_out):
    expert_count = lax.axis_size("expert")
    group_count = lax.axis_size("dp")
    own_index = lax.axis_index("expert")
    tok_rows = tokens.shape[0]
    model_width = tokens.shape[1]
    hidden_units = w_out.shape[1]
    pick_count = expert_ids.shape[1]
    capacity = tok_rows // 8
    slot_count = expert_count * capacity
    pick_rows = tok_rows * pick_count
    half_bit = expert_count.bit_length() - 2
    expert_lane = jnp.arange(expert_count, dtype=jnp.int32)
    partner = jnp.sum(jnp.where(expert_lane == own_index, placement, 0))
    is_moved = partner != own_index
    weight_in = w_in[0]
    weight_out = w_out[0]

    device_hot = (expert_ids.reshape(-1)[:, None] == expert_lane[None, :]).astype(jnp.bfloat16)
    row_lane = jnp.arange(pick_rows, dtype=jnp.int32)
    earlier = (row_lane[None, :] < row_lane[:, None]).astype(jnp.bfloat16)
    slot_rank = jnp.dot(earlier, device_hot, preferred_element_type=jnp.float32).astype(jnp.int32)
    hot = device_hot.astype(jnp.int32)
    slot_place = jnp.sum((slot_rank + expert_lane[None, :] * capacity) * hot, axis=1)
    is_live = jnp.sum(hot, axis=1) > 0
    slot_place = jnp.where(is_live, slot_place, -1).reshape(tok_rows, pick_count)
    slot_hot = slot_place[:, :, None] == jnp.arange(slot_count, dtype=jnp.int32)[None, None, :]
    select = jnp.sum(slot_hot.astype(jnp.bfloat16), axis=1)
    weigh = jnp.sum(jnp.where(slot_hot, gate_weights[:, :, None], 0.0), axis=1)
    slot_gate = jnp.sum(weigh, axis=0)

    send_x = jnp.einsum("ts,td->sd", select, tokens, preferred_element_type=jnp.float32).astype(
        jnp.bfloat16
    )
    send_dy = jnp.einsum("ts,td->sd", select, cotangent, preferred_element_type=jnp.float32)
    send_c = (send_dy * slot_gate[:, None]).astype(jnp.bfloat16)
    arrived = exchange(jnp.concatenate([send_x, send_c], axis=1), expert_count, capacity)
    rows_x = arrived[:, :model_width]
    rows_c = arrived[:, model_width:]

    pre = jnp.dot(rows_x, weight_in, preferred_element_type=jnp.float32)
    gate_pre = pre[:, :hidden_units]
    up_pre = pre[:, hidden_units:]
    sigmoid_gate = jax.nn.sigmoid(gate_pre)
    activated = gate_pre * sigmoid_gate
    hidden = (activated * up_pre).astype(jnp.bfloat16)
    expert_out = jnp.dot(hidden, weight_out, preferred_element_type=jnp.float32).astype(
        jnp.bfloat16
    )
    returned = exchange(expert_out, expert_count, capacity)

    hidden_grad = jnp.einsum("sd,fd->sf", rows_c, weight_out, preferred_element_type=jnp.float32)
    slope = sigmoid_gate * (1.0 + gate_pre * (1.0 - sigmoid_gate))
    gate_up_grad = jnp.concatenate(
        [hidden_grad * up_pre * slope, hidden_grad * activated], axis=1
    ).astype(jnp.bfloat16)
    pick_grad = jnp.einsum(
        "sf,df->sd", gate_up_grad, weight_in, preferred_element_type=jnp.float32
    ).astype(jnp.bfloat16)
    back_grad = exchange(pick_grad, expert_count, capacity)
    in_cols = gate_up_grad.shape[1]
    rest = model_width - in_cols
    part_out = jnp.einsum(
        "sf,sd->fd", hidden, rows_c[:, :in_cols], preferred_element_type=jnp.float32
    ).astype(jnp.bfloat16)
    part_rest = jnp.einsum(
        "sf,sd->fd", hidden, rows_c[:, in_cols:], preferred_element_type=jnp.float32
    ).astype(jnp.bfloat16)
    part_in = jnp.einsum("sd,sf->df", rows_x, gate_up_grad, preferred_element_type=jnp.float32).astype(
        jnp.bfloat16
    )
    in_rows = model_width // group_count
    out_rows = hidden_units // group_count
    rest_as = out_rows * rest // in_cols
    joined = jnp.concatenate(
        [
            part_in.reshape(group_count, in_rows, in_cols),
            part_out.reshape(group_count, out_rows, in_cols),
            part_rest.reshape(group_count, rest_as, in_cols),
        ],
        axis=1,
    ).reshape(group_count * (in_rows + out_rows + rest_as), in_cols)
    returned, back_grad, joined = lax.optimization_barrier((returned, back_grad, joined))
    reduced = lax.psum_scatter(joined, "dp", scatter_dimension=0, tiled=True)

    mixed = jnp.dot(
        weigh,
        returned.astype(jnp.float32),
        precision=lax.Precision.HIGHEST,
        preferred_element_type=jnp.float32,
    ).astype(jnp.bfloat16)
    scores = jnp.einsum("td,sd->ts", cotangent, returned, preferred_element_type=jnp.float32)
    gate_grad = jnp.sum(jnp.where(slot_hot, scores[:, None, :], 0.0), axis=2)
    x_grad = jnp.einsum("ts,sd->td", select, back_grad, preferred_element_type=jnp.float32).astype(
        jnp.bfloat16
    )

    reduced = (reduced.astype(jnp.float32) / group_count).astype(jnp.bfloat16)
    swapped = partner_2(reduced, "expert", half_bit)
    reduced = jnp.where(is_moved, swapped, reduced)
    grad_in = reduced[:in_rows]
    grad_out = jnp.concatenate(
        [reduced[in_rows : in_rows + out_rows], reduced[in_rows + out_rows :].reshape(out_rows, rest)],
        axis=1,
    )
    return (mixed, x_grad, gate_grad, grad_in[None], grad_out[None])


def solution(mesh):
    placed = (
        P(("expert", "dp"), None),
        P(("expert", "dp"), None),
        P(("expert", "dp"), None),
        P(("expert", "dp"), None),
        P(),
        P("expert", None, None),
        P("expert", None, None),
    )
    return jax.shard_map(
        shards,
        mesh=mesh,
        in_specs=placed,
        out_specs=(
            P(("expert", "dp"), None),
            P(("expert", "dp"), None),
            P(("expert", "dp"), None),
            P("expert", "dp", None),
            P("expert", "dp", None),
        ),
        check_vma=False,
    )
```

```python
import jax
import jax.numpy as jnp
from jax import lax
from jax.sharding import PartitionSpec as P


def partner_2(block, axis, apart):
    count = lax.axis_size(axis)
    route = []
    for low in range(count):
        high = low | 1 << apart
        if high != low and high < count:
            route += [(low, high), (high, low)]
    return lax.ppermute(block, axis, route)


def exchange(block, expert_count, capacity):
    shaped = block.reshape(expert_count, capacity, block.shape[-1])
    arrived = lax.all_to_all(shaped, "expert", split_axis=0, concat_axis=0, tiled=True)
    return arrived.reshape(expert_count * capacity, block.shape[-1])


def shards(tokens, cotangent, expert_ids, gate_weights, placement, w_in, w_out):
    expert_count = lax.axis_size("expert")
    group_count = lax.axis_size("dp")
    own_index = lax.axis_index("expert")
    tok_rows = tokens.shape[0]
    model_width = tokens.shape[1]
    hidden_units = w_out.shape[1]
    pick_count = expert_ids.shape[1]
    capacity = tok_rows // 8
    slot_count = expert_count * capacity
    pick_rows = tok_rows * pick_count
    half_bit = expert_count.bit_length() - 2
    expert_lane = jnp.arange(expert_count, dtype=jnp.int32)
    partner = jnp.sum(jnp.where(expert_lane == own_index, placement, 0))
    is_moved = partner != own_index
    weight_in = w_in[0]
    weight_out = w_out[0]

    device_hot = (expert_ids.reshape(-1)[:, None] == expert_lane[None, :]).astype(jnp.bfloat16)
    row_lane = jnp.arange(pick_rows, dtype=jnp.int32)
    earlier = (row_lane[None, :] < row_lane[:, None]).astype(jnp.bfloat16)
    slot_rank = jnp.dot(earlier, device_hot, preferred_element_type=jnp.float32).astype(jnp.int32)
    hot = device_hot.astype(jnp.int32)
    slot_place = jnp.sum((slot_rank + expert_lane[None, :] * capacity) * hot, axis=1)
    is_live = jnp.sum(hot, axis=1) > 0
    slot_place = jnp.where(is_live, slot_place, -1).reshape(tok_rows, pick_count)
    slot_hot = slot_place[:, :, None] == jnp.arange(slot_count, dtype=jnp.int32)[None, None, :]
    select = jnp.sum(slot_hot.astype(jnp.bfloat16), axis=1)
    weigh = jnp.sum(jnp.where(slot_hot, gate_weights[:, :, None], 0.0), axis=1)
    slot_gate = jnp.sum(weigh, axis=0)

    send_x = jnp.einsum("ts,td->sd", select, tokens, preferred_element_type=jnp.float32).astype(
        jnp.bfloat16
    )
    send_dy = jnp.einsum("ts,td->sd", select, cotangent, preferred_element_type=jnp.float32)
    send_c = (send_dy * slot_gate[:, None]).astype(jnp.bfloat16)
    arrived = exchange(jnp.concatenate([send_x, send_c], axis=1), expert_count, capacity)
    rows_x = arrived[:, :model_width]
    rows_c = arrived[:, model_width:]

    pre = jnp.dot(rows_x, weight_in, preferred_element_type=jnp.float32)
    gate_pre = pre[:, :hidden_units]
    up_pre = pre[:, hidden_units:]
    sigmoid_gate = jax.nn.sigmoid(gate_pre)
    activated = gate_pre * sigmoid_gate
    hidden = (activated * up_pre).astype(jnp.bfloat16)
    expert_out = jnp.dot(hidden, weight_out, preferred_element_type=jnp.float32).astype(
        jnp.bfloat16
    )
    returned = exchange(expert_out, expert_count, capacity)

    hidden_grad = jnp.einsum("sd,fd->sf", rows_c, weight_out, preferred_element_type=jnp.float32)
    slope = sigmoid_gate * (1.0 + gate_pre * (1.0 - sigmoid_gate))
    gate_up_grad = jnp.concatenate(
        [hidden_grad * up_pre * slope, hidden_grad * activated], axis=1
    ).astype(jnp.bfloat16)
    pick_grad = jnp.einsum(
        "sf,df->sd", gate_up_grad, weight_in, preferred_element_type=jnp.float32
    ).astype(jnp.bfloat16)
    in_cols = gate_up_grad.shape[1]
    rest = model_width - in_cols
    in_rows = model_width // group_count
    out_rows = hidden_units // group_count
    rest_rows = out_rows // (in_cols // rest)
    scale = 1.0 / group_count
    part_out = (
        jnp.einsum("sf,sd->fd", hidden, rows_c, preferred_element_type=jnp.float32) * scale
    ).astype(jnp.bfloat16).reshape(group_count, out_rows, model_width)
    part_in = (
        jnp.einsum("sd,sf->df", rows_x, gate_up_grad, preferred_element_type=jnp.float32) * scale
    ).astype(jnp.bfloat16).reshape(group_count, in_rows, in_cols)
    tail = part_out[:, :, in_cols:]
    bands = [tail[:, k * rest_rows : (k + 1) * rest_rows] for k in range(in_cols // rest)]
    joined = jnp.concatenate(
        [part_in, part_out[:, :, :in_cols], jnp.concatenate(bands, axis=2)], axis=1
    ).reshape(group_count * (in_rows + out_rows + rest_rows), in_cols)
    returned, joined = lax.optimization_barrier((returned, joined))
    reduced = lax.psum_scatter(joined, "dp", scatter_dimension=0, tiled=True)
    reduced, pick_grad = lax.optimization_barrier((reduced, pick_grad))
    back_grad = exchange(pick_grad, expert_count, capacity)

    mixed = jnp.dot(
        weigh,
        returned.astype(jnp.float32),
        precision=lax.Precision.HIGHEST,
        preferred_element_type=jnp.float32,
    ).astype(jnp.bfloat16)
    scores = jnp.einsum("td,sd->ts", cotangent, returned, preferred_element_type=jnp.float32)
    gate_grad = jnp.sum(jnp.where(slot_hot, scores[:, None, :], 0.0), axis=2)
    x_grad = jnp.einsum("ts,sd->td", select, back_grad, preferred_element_type=jnp.float32).astype(
        jnp.bfloat16
    )

    swapped = partner_2(reduced, "expert", half_bit)
    reduced = jnp.where(is_moved, swapped, reduced)
    grad_in = reduced[:in_rows]
    tail = reduced[in_rows + out_rows :]
    grad_out = jnp.concatenate(
        [reduced[in_rows : in_rows + out_rows],
         jnp.concatenate([tail[:, k * rest : (k + 1) * rest] for k in range(in_cols // rest)], axis=0)],
        axis=1,
    )
    return (mixed, x_grad, gate_grad, grad_in[None], grad_out[None])


def solution(mesh):
    placed = (
        P(("expert", "dp"), None),
        P(("expert", "dp"), None),
        P(("expert", "dp"), None),
        P(("expert", "dp"), None),
        P(),
        P("expert", None, None),
        P("expert", None, None),
    )
    return jax.shard_map(
        shards,
        mesh=mesh,
        in_specs=placed,
        out_specs=(
            P(("expert", "dp"), None),
            P(("expert", "dp"), None),
            P(("expert", "dp"), None),
            P("expert", "dp", None),
            P("expert", "dp", None),
        ),
        check_vma=False,
    )
```

```python
import jax
import jax.numpy as jnp
from jax import lax
from jax.sharding import PartitionSpec as P


def partner_2(block, axis, apart):
    count = lax.axis_size(axis)
    route = []
    for low in range(count):
        high = low | 1 << apart
        if high != low and high < count:
            route += [(low, high), (high, low)]
    return lax.ppermute(block, axis, route)


def pair_groups(expert_count, group_count):
    half = group_count // 2
    groups = []
    for flip in range(2):
        for z in range(half):
            members = []
            for e in range(expert_count):
                x_lo = flip ^ ((e >> 1) & 1)
                members.append(e * group_count + x_lo * half + z)
            groups.append(members)
    return groups


def exchange(block, expert_count, capacity):
    group_count = lax.axis_size("dp")
    shaped = block.reshape(expert_count, capacity, block.shape[-1])
    arrived = lax.all_to_all(
        shaped,
        ("expert", "dp"),
        split_axis=0,
        concat_axis=0,
        tiled=True,
        axis_index_groups=pair_groups(expert_count, group_count),
    )
    return arrived.reshape(expert_count * capacity, block.shape[-1])


def shards(tokens, cotangent, expert_ids, gate_weights, placement, w_in, w_out):
    expert_count = lax.axis_size("expert")
    group_count = lax.axis_size("dp")
    own_index = lax.axis_index("expert")
    tok_rows = tokens.shape[0]
    model_width = tokens.shape[1]
    hidden_units = w_out.shape[1]
    pick_count = expert_ids.shape[1]
    capacity = tok_rows // 8
    slot_count = expert_count * capacity
    pick_rows = tok_rows * pick_count
    half_bit = expert_count.bit_length() - 2
    expert_lane = jnp.arange(expert_count, dtype=jnp.int32)
    partner = jnp.sum(jnp.where(expert_lane == own_index, placement, 0))
    is_moved = partner != own_index
    weight_in = w_in[0]
    weight_out = w_out[0]

    device_hot = (expert_ids.reshape(-1)[:, None] == expert_lane[None, :]).astype(jnp.bfloat16)
    row_lane = jnp.arange(pick_rows, dtype=jnp.int32)
    earlier = (row_lane[None, :] < row_lane[:, None]).astype(jnp.bfloat16)
    slot_rank = jnp.dot(earlier, device_hot, preferred_element_type=jnp.float32).astype(jnp.int32)
    hot = device_hot.astype(jnp.int32)
    slot_place = jnp.sum((slot_rank + expert_lane[None, :] * capacity) * hot, axis=1)
    is_live = jnp.sum(hot, axis=1) > 0
    slot_place = jnp.where(is_live, slot_place, -1).reshape(tok_rows, pick_count)
    slot_hot = slot_place[:, :, None] == jnp.arange(slot_count, dtype=jnp.int32)[None, None, :]
    select = jnp.sum(slot_hot.astype(jnp.bfloat16), axis=1)
    weigh = jnp.sum(jnp.where(slot_hot, gate_weights[:, :, None], 0.0), axis=1)
    slot_gate = jnp.sum(weigh, axis=0)

    send_x = jnp.einsum("ts,td->sd", select, tokens, preferred_element_type=jnp.float32).astype(
        jnp.bfloat16
    )
    send_dy = jnp.einsum("ts,td->sd", select, cotangent, preferred_element_type=jnp.float32)
    send_c = (send_dy * slot_gate[:, None]).astype(jnp.bfloat16)
    arrived = exchange(jnp.concatenate([send_x, send_c], axis=1), expert_count, capacity)
    rows_x = arrived[:, :model_width]
    rows_c = arrived[:, model_width:]

    pre = jnp.dot(rows_x, weight_in, preferred_element_type=jnp.float32)
    gate_pre = pre[:, :hidden_units]
    up_pre = pre[:, hidden_units:]
    sigmoid_gate = jax.nn.sigmoid(gate_pre)
    activated = gate_pre * sigmoid_gate
    hidden = (activated * up_pre).astype(jnp.bfloat16)
    expert_out = jnp.dot(hidden, weight_out, preferred_element_type=jnp.float32).astype(
        jnp.bfloat16
    )
    returned = exchange(expert_out, expert_count, capacity)

    hidden_grad = jnp.einsum("sd,fd->sf", rows_c, weight_out, preferred_element_type=jnp.float32)
    slope = sigmoid_gate * (1.0 + gate_pre * (1.0 - sigmoid_gate))
    gate_up_grad = jnp.concatenate(
        [hidden_grad * up_pre * slope, hidden_grad * activated], axis=1
    ).astype(jnp.bfloat16)
    pick_grad = jnp.einsum(
        "sf,df->sd", gate_up_grad, weight_in, preferred_element_type=jnp.float32
    ).astype(jnp.bfloat16)
    in_cols = gate_up_grad.shape[1]
    rest = model_width - in_cols
    in_rows = model_width // group_count
    out_rows = hidden_units // group_count
    rest_rows = out_rows // (in_cols // rest)
    scale = 1.0 / group_count
    part_out = (
        jnp.einsum("sf,sd->fd", hidden, rows_c, preferred_element_type=jnp.float32) * scale
    ).astype(jnp.bfloat16).reshape(group_count, out_rows, model_width)
    part_in = (
        jnp.einsum("sd,sf->df", rows_x, gate_up_grad, preferred_element_type=jnp.float32) * scale
    ).astype(jnp.bfloat16).reshape(group_count, in_rows, in_cols)
    tail = part_out[:, :, in_cols:]
    bands = [tail[:, k * rest_rows : (k + 1) * rest_rows] for k in range(in_cols // rest)]
    joined = jnp.concatenate(
        [part_in, part_out[:, :, :in_cols], jnp.concatenate(bands, axis=2)], axis=1
    ).reshape(group_count * (in_rows + out_rows + rest_rows), in_cols)
    returned, joined = lax.optimization_barrier((returned, joined))
    reduced = lax.psum_scatter(joined, "dp", scatter_dimension=0, tiled=True)
    reduced, pick_grad = lax.optimization_barrier((reduced, pick_grad))
    back_grad = exchange(pick_grad, expert_count, capacity)

    mixed = jnp.dot(
        weigh,
        returned.astype(jnp.float32),
        precision=lax.Precision.HIGHEST,
        preferred_element_type=jnp.float32,
    ).astype(jnp.bfloat16)
    scores = jnp.einsum("td,sd->ts", cotangent, returned, preferred_element_type=jnp.float32)
    gate_grad = jnp.sum(jnp.where(slot_hot, scores[:, None, :], 0.0), axis=2)
    x_grad = jnp.einsum("ts,sd->td", select, back_grad, preferred_element_type=jnp.float32).astype(
        jnp.bfloat16
    )

    swapped = partner_2(reduced, "expert", half_bit)
    reduced = jnp.where(is_moved, swapped, reduced)
    grad_in = reduced[:in_rows]
    tail = reduced[in_rows + out_rows :]
    grad_out = jnp.concatenate(
        [reduced[in_rows : in_rows + out_rows],
         jnp.concatenate([tail[:, k * rest : (k + 1) * rest] for k in range(in_cols // rest)], axis=0)],
        axis=1,
    )
    return (mixed, x_grad, gate_grad, grad_in[None], grad_out[None])


def solution(mesh):
    placed = (
        P(("expert", "dp"), None),
        P(("expert", "dp"), None),
        P(("expert", "dp"), None),
        P(("expert", "dp"), None),
        P(),
        P("expert", None, None),
        P("expert", None, None),
    )
    return jax.shard_map(
        shards,
        mesh=mesh,
        in_specs=placed,
        out_specs=(
            P(("expert", "dp"), None),
            P(("expert", "dp"), None),
            P(("expert", "dp"), None),
            P("expert", "dp", None),
            P("expert", "dp", None),
        ),
        check_vma=False,
    )
```

```python
import jax
import jax.numpy as jnp
from jax import lax
from jax.sharding import PartitionSpec as P


def partner_2(block, axis, apart):
    count = lax.axis_size(axis)
    route = []
    for low in range(count):
        high = low | 1 << apart
        if high != low and high < count:
            route += [(low, high), (high, low)]
    return lax.ppermute(block, axis, route)


def pair_groups(expert_count, group_count):
    half = group_count // 2
    groups = []
    for flip in range(2):
        for z in range(half):
            members = []
            for e in range(expert_count):
                x_lo = flip ^ ((e >> 1) & 1)
                members.append(e * group_count + x_lo * half + z)
            groups.append(members)
    return groups


def exchange(block, expert_count, capacity):
    group_count = lax.axis_size("dp")
    shaped = block.reshape(expert_count, capacity, block.shape[-1])
    arrived = lax.all_to_all(
        shaped,
        ("expert", "dp"),
        split_axis=0,
        concat_axis=0,
        tiled=True,
        axis_index_groups=pair_groups(expert_count, group_count),
    )
    return arrived.reshape(expert_count * capacity, block.shape[-1])


def shards(tokens, cotangent, expert_ids, gate_weights, placement, w_in, w_out):
    expert_count = lax.axis_size("expert")
    group_count = lax.axis_size("dp")
    own_index = lax.axis_index("expert")
    tok_rows = tokens.shape[0]
    model_width = tokens.shape[1]
    hidden_units = w_out.shape[1]
    pick_count = expert_ids.shape[1]
    capacity = tok_rows // 8
    slot_count = expert_count * capacity
    pick_rows = tok_rows * pick_count
    half_bit = expert_count.bit_length() - 2
    expert_lane = jnp.arange(expert_count, dtype=jnp.int32)
    partner = jnp.sum(jnp.where(expert_lane == own_index, placement, 0))
    is_moved = partner != own_index
    weight_in = w_in[0]
    weight_out = w_out[0]

    device_hot = (expert_ids.reshape(-1)[:, None] == expert_lane[None, :]).astype(jnp.bfloat16)
    row_lane = jnp.arange(pick_rows, dtype=jnp.int32)
    earlier = (row_lane[None, :] < row_lane[:, None]).astype(jnp.bfloat16)
    slot_rank = jnp.dot(earlier, device_hot, preferred_element_type=jnp.float32).astype(jnp.int32)
    hot = device_hot.astype(jnp.int32)
    slot_place = jnp.sum((slot_rank + expert_lane[None, :] * capacity) * hot, axis=1)
    is_live = jnp.sum(hot, axis=1) > 0
    slot_place = jnp.where(is_live, slot_place, -1).reshape(tok_rows, pick_count)
    slot_hot = slot_place[:, :, None] == jnp.arange(slot_count, dtype=jnp.int32)[None, None, :]
    select = jnp.sum(slot_hot.astype(jnp.bfloat16), axis=1)
    weigh = jnp.sum(jnp.where(slot_hot, gate_weights[:, :, None], 0.0), axis=1)
    slot_gate = jnp.sum(weigh, axis=0)

    send_x = jnp.einsum("ts,td->sd", select, tokens, preferred_element_type=jnp.float32).astype(
        jnp.bfloat16
    )
    send_dy = jnp.einsum("ts,td->sd", select, cotangent, preferred_element_type=jnp.float32)
    send_c = (send_dy * slot_gate[:, None]).astype(jnp.bfloat16)
    arrived = exchange(jnp.concatenate([send_x, send_c], axis=1), expert_count, capacity)
    rows_x = arrived[:, :model_width]
    rows_c = arrived[:, model_width:]

    pre = jnp.dot(rows_x, weight_in, preferred_element_type=jnp.float32)
    gate_pre = pre[:, :hidden_units]
    up_pre = pre[:, hidden_units:]
    sigmoid_gate = jax.nn.sigmoid(gate_pre)
    activated = gate_pre * sigmoid_gate
    hidden = (activated * up_pre).astype(jnp.bfloat16)
    expert_out = jnp.dot(hidden, weight_out, preferred_element_type=jnp.float32).astype(
        jnp.bfloat16
    )
    returned = exchange(expert_out, expert_count, capacity)

    hidden_grad = jnp.einsum("sd,fd->sf", rows_c, weight_out, preferred_element_type=jnp.float32)
    slope = sigmoid_gate * (1.0 + gate_pre * (1.0 - sigmoid_gate))
    gate_up_grad = jnp.concatenate(
        [hidden_grad * up_pre * slope, hidden_grad * activated], axis=1
    ).astype(jnp.bfloat16)
    pick_grad = jnp.einsum(
        "sf,df->sd", gate_up_grad, weight_in, preferred_element_type=jnp.float32
    ).astype(jnp.bfloat16)
    in_cols = gate_up_grad.shape[1]
    rest = model_width - in_cols
    in_rows = model_width // group_count
    out_rows = hidden_units // group_count
    rest_rows = out_rows // (in_cols // rest)
    scale = 1.0 / group_count
    part_out = (
        jnp.einsum("sf,sd->fd", hidden, rows_c, preferred_element_type=jnp.float32) * scale
    ).astype(jnp.bfloat16).reshape(group_count, out_rows, model_width)
    part_in = (
        jnp.einsum("sd,sf->df", rows_x, gate_up_grad, preferred_element_type=jnp.float32) * scale
    ).astype(jnp.bfloat16).reshape(group_count, in_rows, in_cols)
    tail = part_out[:, :, in_cols:]
    bands = [tail[:, k * rest_rows : (k + 1) * rest_rows] for k in range(in_cols // rest)]
    joined = jnp.concatenate(
        [part_in, part_out[:, :, :in_cols], jnp.concatenate(bands, axis=2)], axis=1
    ).reshape(group_count * (in_rows + out_rows + rest_rows), in_cols)
    reduced = lax.psum_scatter(joined, "dp", scatter_dimension=0, tiled=True)
    back_grad = exchange(pick_grad, expert_count, capacity)

    mixed = jnp.dot(
        weigh,
        returned.astype(jnp.float32),
        precision=lax.Precision.HIGHEST,
        preferred_element_type=jnp.float32,
    ).astype(jnp.bfloat16)
    scores = jnp.einsum("td,sd->ts", cotangent, returned, preferred_element_type=jnp.float32)
    gate_grad = jnp.sum(jnp.where(slot_hot, scores[:, None, :], 0.0), axis=2)
    x_grad = jnp.einsum("ts,sd->td", select, back_grad, preferred_element_type=jnp.float32).astype(
        jnp.bfloat16
    )

    swapped = partner_2(reduced, "expert", half_bit)
    reduced = jnp.where(is_moved, swapped, reduced)
    grad_in = reduced[:in_rows]
    tail = reduced[in_rows + out_rows :]
    grad_out = jnp.concatenate(
        [reduced[in_rows : in_rows + out_rows],
         jnp.concatenate([tail[:, k * rest : (k + 1) * rest] for k in range(in_cols // rest)], axis=0)],
        axis=1,
    )
    return (mixed, x_grad, gate_grad, grad_in[None], grad_out[None])


def solution(mesh):
    placed = (
        P(("expert", "dp"), None),
        P(("expert", "dp"), None),
        P(("expert", "dp"), None),
        P(("expert", "dp"), None),
        P(),
        P("expert", None, None),
        P("expert", None, None),
    )
    return jax.shard_map(
        shards,
        mesh=mesh,
        in_specs=placed,
        out_specs=(
            P(("expert", "dp"), None),
            P(("expert", "dp"), None),
            P(("expert", "dp"), None),
            P("expert", "dp", None),
            P("expert", "dp", None),
        ),
        check_vma=False,
    )
```

```python
import jax
import jax.numpy as jnp
from jax import lax
from jax.sharding import PartitionSpec as P


def partner_2(block, axis, apart):
    count = lax.axis_size(axis)
    route = []
    for low in range(count):
        high = low | 1 << apart
        if high != low and high < count:
            route += [(low, high), (high, low)]
    return lax.ppermute(block, axis, route)


def pair_groups(expert_count, group_count):
    half = group_count // 2
    groups = []
    for flip in range(2):
        for z in range(half):
            members = []
            for e in range(expert_count):
                x_lo = flip ^ ((e >> 1) & 1)
                members.append(e * group_count + x_lo * half + z)
            groups.append(members)
    return groups


def exchange(block, expert_count, capacity):
    group_count = lax.axis_size("dp")
    shaped = block.reshape(expert_count, capacity, block.shape[-1])
    arrived = lax.all_to_all(
        shaped,
        ("expert", "dp"),
        split_axis=0,
        concat_axis=0,
        tiled=True,
        axis_index_groups=pair_groups(expert_count, group_count),
    )
    return arrived.reshape(expert_count * capacity, block.shape[-1])


def shards(tokens, cotangent, expert_ids, gate_weights, placement, w_in, w_out):
    expert_count = lax.axis_size("expert")
    group_count = lax.axis_size("dp")
    own_index = lax.axis_index("expert")
    tok_rows = tokens.shape[0]
    model_width = tokens.shape[1]
    hidden_units = w_out.shape[1]
    pick_count = expert_ids.shape[1]
    capacity = tok_rows // 8
    slot_count = expert_count * capacity
    pick_rows = tok_rows * pick_count
    half_bit = expert_count.bit_length() - 2
    expert_lane = jnp.arange(expert_count, dtype=jnp.int32)
    partner = jnp.sum(jnp.where(expert_lane == own_index, placement, 0))
    is_moved = partner != own_index
    weight_in = w_in[0]
    weight_out = w_out[0]

    device_hot = (expert_ids.reshape(-1)[:, None] == expert_lane[None, :]).astype(jnp.bfloat16)
    row_lane = jnp.arange(pick_rows, dtype=jnp.int32)
    earlier = (row_lane[None, :] < row_lane[:, None]).astype(jnp.bfloat16)
    slot_rank = jnp.dot(earlier, device_hot, preferred_element_type=jnp.float32).astype(jnp.int32)
    hot = device_hot.astype(jnp.int32)
    slot_place = jnp.sum((slot_rank + expert_lane[None, :] * capacity) * hot, axis=1)
    is_live = jnp.sum(hot, axis=1) > 0
    slot_place = jnp.where(is_live, slot_place, -1).reshape(tok_rows, pick_count)
    slot_hot = slot_place[:, :, None] == jnp.arange(slot_count, dtype=jnp.int32)[None, None, :]
    select = jnp.sum(slot_hot.astype(jnp.bfloat16), axis=1)
    weigh = jnp.sum(jnp.where(slot_hot, gate_weights[:, :, None], 0.0), axis=1)
    slot_gate = jnp.sum(weigh, axis=0)

    send_x = jnp.einsum("ts,td->sd", select, tokens, preferred_element_type=jnp.float32).astype(
        jnp.bfloat16
    )
    send_dy = jnp.einsum("ts,td->sd", select, cotangent, preferred_element_type=jnp.float32)
    send_c = (send_dy * slot_gate[:, None]).astype(jnp.bfloat16)
    arrived = exchange(jnp.concatenate([send_x, send_c], axis=1), expert_count, capacity)
    rows_x = arrived[:, :model_width]
    rows_c = arrived[:, model_width:]

    pre = jnp.dot(rows_x, weight_in, preferred_element_type=jnp.float32)
    gate_pre = pre[:, :hidden_units]
    up_pre = pre[:, hidden_units:]
    sigmoid_gate = jax.nn.sigmoid(gate_pre)
    activated = gate_pre * sigmoid_gate
    hidden = (activated * up_pre).astype(jnp.bfloat16)
    expert_out = jnp.dot(hidden, weight_out, preferred_element_type=jnp.float32).astype(
        jnp.bfloat16
    )
    returned = exchange(expert_out, expert_count, capacity)

    hidden_grad = jnp.einsum("sd,fd->sf", rows_c, weight_out, preferred_element_type=jnp.float32)
    slope = sigmoid_gate * (1.0 + gate_pre * (1.0 - sigmoid_gate))
    gate_up_grad = jnp.concatenate(
        [hidden_grad * up_pre * slope, hidden_grad * activated], axis=1
    ).astype(jnp.bfloat16)
    pick_grad = jnp.einsum(
        "sf,df->sd", gate_up_grad, weight_in, preferred_element_type=jnp.float32
    ).astype(jnp.bfloat16)
    in_cols = gate_up_grad.shape[1]
    rest = model_width - in_cols
    in_rows = model_width // group_count
    out_rows = hidden_units // group_count
    rest_rows = out_rows // (in_cols // rest)
    scale = 1.0 / group_count
    part_out = (
        jnp.einsum("sf,sd->fd", hidden, rows_c, preferred_element_type=jnp.float32) * scale
    ).astype(jnp.bfloat16).reshape(group_count, out_rows, model_width)
    part_in = (
        jnp.einsum("sd,sf->df", rows_x, gate_up_grad, preferred_element_type=jnp.float32) * scale
    ).astype(jnp.bfloat16).reshape(group_count, in_rows, in_cols)
    tail = part_out[:, :, in_cols:]
    bands = [tail[:, k * rest_rows : (k + 1) * rest_rows] for k in range(in_cols // rest)]
    joined = jnp.concatenate(
        [part_in, part_out[:, :, :in_cols], jnp.concatenate(bands, axis=2)], axis=1
    ).reshape(group_count * (in_rows + out_rows + rest_rows), in_cols)
    reduced = lax.psum_scatter(joined, "dp", scatter_dimension=0, tiled=True)
    back_grad = exchange(pick_grad, expert_count, capacity)

    mixed = jnp.dot(
        weigh,
        returned.astype(jnp.float32),
        precision=lax.Precision.HIGHEST,
        preferred_element_type=jnp.float32,
    ).astype(jnp.bfloat16)
    scores = jnp.einsum("td,sd->ts", cotangent, returned, preferred_element_type=jnp.float32)
    gate_grad = jnp.sum(jnp.where(slot_hot, scores[:, None, :], 0.0), axis=2)
    x_grad = jnp.einsum("ts,sd->td", select, back_grad, preferred_element_type=jnp.float32).astype(
        jnp.bfloat16
    )

    mixed, x_grad, gate_grad, reduced = lax.optimization_barrier((mixed, x_grad, gate_grad, reduced))
    swapped = partner_2(reduced, "expert", half_bit)
    reduced = jnp.where(is_moved, swapped, reduced)
    grad_in = reduced[:in_rows]
    tail = reduced[in_rows + out_rows :]
    grad_out = jnp.concatenate(
        [reduced[in_rows : in_rows + out_rows],
         jnp.concatenate([tail[:, k * rest : (k + 1) * rest] for k in range(in_cols // rest)], axis=0)],
        axis=1,
    )
    return (mixed, x_grad, gate_grad, grad_in[None], grad_out[None])


def solution(mesh):
    placed = (
        P(("expert", "dp"), None),
        P(("expert", "dp"), None),
        P(("expert", "dp"), None),
        P(("expert", "dp"), None),
        P(),
        P("expert", None, None),
        P("expert", None, None),
    )
    return jax.shard_map(
        shards,
        mesh=mesh,
        in_specs=placed,
        out_specs=(
            P(("expert", "dp"), None),
            P(("expert", "dp"), None),
            P(("expert", "dp"), None),
            P("expert", "dp", None),
            P("expert", "dp", None),
        ),
        check_vma=False,
    )
```

```python
import jax
import jax.numpy as jnp
from jax import lax
from jax.experimental import pallas as pl
from jax.sharding import PartitionSpec as P


def partner_2(block, axis, apart):
    count = lax.axis_size(axis)
    route = []
    for low in range(count):
        high = low | 1 << apart
        if high != low and high < count:
            route += [(low, high), (high, low)]
    return lax.ppermute(block, axis, route)


def joined_grads(x_t, gate_up_grad, hidden_t, rows_c, groups, scale):
    model_width, slots = x_t.shape
    in_cols = gate_up_grad.shape[1]
    hidden_units = hidden_t.shape[0]
    in_rows = model_width // groups
    out_rows = hidden_units // groups
    rest = model_width - in_cols
    bands = in_cols // rest
    rest_rows = out_rows // bands
    total = in_rows + out_rows + rest_rows

    def body(x_ref, gu_ref, h_ref, c_ref, o_ref):
        part_in = jnp.dot(x_ref[...], gu_ref[...], preferred_element_type=jnp.float32) * scale
        o_ref[0, 0:in_rows, :] = part_in.astype(o_ref.dtype)
        h = h_ref[...]
        part_out = jnp.dot(h, c_ref[:, 0:in_cols], preferred_element_type=jnp.float32) * scale
        o_ref[0, in_rows : in_rows + out_rows, :] = part_out.astype(o_ref.dtype)
        tail = jnp.dot(h, c_ref[:, in_cols:], preferred_element_type=jnp.float32) * scale
        for k in range(bands):
            o_ref[0, in_rows + out_rows :, k * rest : (k + 1) * rest] = tail[
                k * rest_rows : (k + 1) * rest_rows
            ].astype(o_ref.dtype)

    flops = 2 * slots * (model_width * in_cols + hidden_units * model_width)
    return pl.pallas_call(
        body,
        out_shape=jax.ShapeDtypeStruct((groups, total, in_cols), jnp.bfloat16),
        grid=(groups,),
        in_specs=[
            pl.BlockSpec((in_rows, slots), lambda g: (g, 0)),
            pl.BlockSpec((slots, in_cols), lambda g: (0, 0)),
            pl.BlockSpec((out_rows, slots), lambda g: (g, 0)),
            pl.BlockSpec((slots, model_width), lambda g: (0, 0)),
        ],
        out_specs=pl.BlockSpec((1, total, in_cols), lambda g: (g, 0, 0)),
        cost_estimate=pl.CostEstimate(
            flops=flops, transcendentals=0,
            bytes_accessed=2 * (slots * (2 * model_width + in_cols + hidden_units) + groups * total * in_cols),
        ),
    )(x_t, gate_up_grad, hidden_t, rows_c)


def pair_groups(expert_count, group_count):
    half = group_count // 2
    groups = []
    for flip in range(2):
        for z in range(half):
            members = []
            for e in range(expert_count):
                x_lo = flip ^ ((e >> 1) & 1)
                members.append(e * group_count + x_lo * half + z)
            groups.append(members)
    return groups


def exchange(block, expert_count, capacity):
    group_count = lax.axis_size("dp")
    shaped = block.reshape(expert_count, capacity, block.shape[-1])
    arrived = lax.all_to_all(
        shaped,
        ("expert", "dp"),
        split_axis=0,
        concat_axis=0,
        tiled=True,
        axis_index_groups=pair_groups(expert_count, group_count),
    )
    return arrived.reshape(expert_count * capacity, block.shape[-1])


def shards(tokens, cotangent, expert_ids, gate_weights, placement, w_in, w_out):
    expert_count = lax.axis_size("expert")
    group_count = lax.axis_size("dp")
    own_index = lax.axis_index("expert")
    tok_rows = tokens.shape[0]
    model_width = tokens.shape[1]
    hidden_units = w_out.shape[1]
    pick_count = expert_ids.shape[1]
    capacity = tok_rows // 8
    slot_count = expert_count * capacity
    pick_rows = tok_rows * pick_count
    half_bit = expert_count.bit_length() - 2
    expert_lane = jnp.arange(expert_count, dtype=jnp.int32)
    partner = jnp.sum(jnp.where(expert_lane == own_index, placement, 0))
    is_moved = partner != own_index
    weight_in = w_in[0]
    weight_out = w_out[0]

    device_hot = (expert_ids.reshape(-1)[:, None] == expert_lane[None, :]).astype(jnp.bfloat16)
    row_lane = jnp.arange(pick_rows, dtype=jnp.int32)
    earlier = (row_lane[None, :] < row_lane[:, None]).astype(jnp.bfloat16)
    slot_rank = jnp.dot(earlier, device_hot, preferred_element_type=jnp.float32).astype(jnp.int32)
    hot = device_hot.astype(jnp.int32)
    slot_place = jnp.sum((slot_rank + expert_lane[None, :] * capacity) * hot, axis=1)
    is_live = jnp.sum(hot, axis=1) > 0
    slot_place = jnp.where(is_live, slot_place, -1).reshape(tok_rows, pick_count)
    slot_hot = slot_place[:, :, None] == jnp.arange(slot_count, dtype=jnp.int32)[None, None, :]
    select = jnp.sum(slot_hot.astype(jnp.bfloat16), axis=1)
    weigh = jnp.sum(jnp.where(slot_hot, gate_weights[:, :, None], 0.0), axis=1)
    slot_gate = jnp.sum(weigh, axis=0)

    send_x = jnp.einsum("ts,td->sd", select, tokens, preferred_element_type=jnp.float32).astype(
        jnp.bfloat16
    )
    send_dy = jnp.einsum("ts,td->sd", select, cotangent, preferred_element_type=jnp.float32)
    send_c = (send_dy * slot_gate[:, None]).astype(jnp.bfloat16)
    arrived = exchange(jnp.concatenate([send_x, send_c], axis=1), expert_count, capacity)
    rows_x = arrived[:, :model_width]
    rows_c = arrived[:, model_width:]

    pre = jnp.dot(rows_x, weight_in, preferred_element_type=jnp.float32)
    gate_pre = pre[:, :hidden_units]
    up_pre = pre[:, hidden_units:]
    sigmoid_gate = jax.nn.sigmoid(gate_pre)
    activated = gate_pre * sigmoid_gate
    hidden = (activated * up_pre).astype(jnp.bfloat16)
    expert_out = jnp.dot(hidden, weight_out, preferred_element_type=jnp.float32).astype(
        jnp.bfloat16
    )
    returned = exchange(expert_out, expert_count, capacity)

    hidden_grad = jnp.einsum("sd,fd->sf", rows_c, weight_out, preferred_element_type=jnp.float32)
    slope = sigmoid_gate * (1.0 + gate_pre * (1.0 - sigmoid_gate))
    gate_up_grad = jnp.concatenate(
        [hidden_grad * up_pre * slope, hidden_grad * activated], axis=1
    ).astype(jnp.bfloat16)
    pick_grad = jnp.einsum(
        "sf,df->sd", gate_up_grad, weight_in, preferred_element_type=jnp.float32
    ).astype(jnp.bfloat16)
    in_cols = gate_up_grad.shape[1]
    rest = model_width - in_cols
    in_rows = model_width // group_count
    out_rows = hidden_units // group_count
    rest_rows = out_rows // (in_cols // rest)
    scale = 1.0 / group_count
    joined = joined_grads(rows_x.T, gate_up_grad, hidden.T, rows_c, group_count, scale)
    joined = joined.reshape(group_count * joined.shape[1], in_cols)
    reduced = lax.psum_scatter(joined, "dp", scatter_dimension=0, tiled=True)
    back_grad = exchange(pick_grad, expert_count, capacity)

    mixed = jnp.dot(
        weigh,
        returned.astype(jnp.float32),
        precision=lax.Precision.HIGHEST,
        preferred_element_type=jnp.float32,
    ).astype(jnp.bfloat16)
    scores = jnp.einsum("td,sd->ts", cotangent, returned, preferred_element_type=jnp.float32)
    gate_grad = jnp.sum(jnp.where(slot_hot, scores[:, None, :], 0.0), axis=2)
    x_grad = jnp.einsum("ts,sd->td", select, back_grad, preferred_element_type=jnp.float32).astype(
        jnp.bfloat16
    )

    mixed, x_grad, gate_grad, reduced = lax.optimization_barrier((mixed, x_grad, gate_grad, reduced))
    swapped = partner_2(reduced, "expert", half_bit)
    reduced = jnp.where(is_moved, swapped, reduced)
    grad_in = reduced[:in_rows]
    tail = reduced[in_rows + out_rows :]
    grad_out = jnp.concatenate(
        [reduced[in_rows : in_rows + out_rows],
         jnp.concatenate([tail[:, k * rest : (k + 1) * rest] for k in range(in_cols // rest)], axis=0)],
        axis=1,
    )
    return (mixed, x_grad, gate_grad, grad_in[None], grad_out[None])


def solution(mesh):
    placed = (
        P(("expert", "dp"), None),
        P(("expert", "dp"), None),
        P(("expert", "dp"), None),
        P(("expert", "dp"), None),
        P(),
        P("expert", None, None),
        P("expert", None, None),
    )
    return jax.shard_map(
        shards,
        mesh=mesh,
        in_specs=placed,
        out_specs=(
            P(("expert", "dp"), None),
            P(("expert", "dp"), None),
            P(("expert", "dp"), None),
            P("expert", "dp", None),
            P("expert", "dp", None),
        ),
        check_vma=False,
    )
```

```python
import jax
import jax.numpy as jnp
from jax import lax
from jax.sharding import PartitionSpec as P


def partner_2(block, axis, apart):
    count = lax.axis_size(axis)
    route = []
    for low in range(count):
        high = low | 1 << apart
        if high != low and high < count:
            route += [(low, high), (high, low)]
    return lax.ppermute(block, axis, route)


def pair_groups(expert_count, group_count):
    half = group_count // 2
    groups = []
    for flip in range(2):
        for z in range(half):
            members = []
            for e in range(expert_count):
                x_lo = flip ^ ((e >> 1) & 1)
                members.append(e * group_count + x_lo * half + z)
            groups.append(members)
    return groups


def exchange(block, expert_count, capacity):
    group_count = lax.axis_size("dp")
    shaped = block.reshape(expert_count, capacity, block.shape[-1])
    arrived = lax.all_to_all(
        shaped,
        ("expert", "dp"),
        split_axis=0,
        concat_axis=0,
        tiled=True,
        axis_index_groups=pair_groups(expert_count, group_count),
    )
    return arrived.reshape(expert_count * capacity, block.shape[-1])


def shards(tokens, cotangent, expert_ids, gate_weights, placement, w_in, w_out):
    expert_count = lax.axis_size("expert")
    group_count = lax.axis_size("dp")
    own_index = lax.axis_index("expert")
    tok_rows = tokens.shape[0]
    model_width = tokens.shape[1]
    hidden_units = w_out.shape[1]
    pick_count = expert_ids.shape[1]
    capacity = tok_rows // 8
    slot_count = expert_count * capacity
    pick_rows = tok_rows * pick_count
    half_bit = expert_count.bit_length() - 2
    expert_lane = jnp.arange(expert_count, dtype=jnp.int32)
    partner = jnp.sum(jnp.where(expert_lane == own_index, placement, 0))
    is_moved = partner != own_index
    weight_in = w_in[0]
    weight_out = w_out[0]

    device_hot = (expert_ids.reshape(-1)[:, None] == expert_lane[None, :]).astype(jnp.bfloat16)
    row_lane = jnp.arange(pick_rows, dtype=jnp.int32)
    earlier = (row_lane[None, :] < row_lane[:, None]).astype(jnp.bfloat16)
    slot_rank = jnp.dot(earlier, device_hot, preferred_element_type=jnp.float32).astype(jnp.int32)
    hot = device_hot.astype(jnp.int32)
    slot_place = jnp.sum((slot_rank + expert_lane[None, :] * capacity) * hot, axis=1)
    is_live = jnp.sum(hot, axis=1) > 0
    slot_place = jnp.where(is_live, slot_place, -1).reshape(tok_rows, pick_count)
    slot_hot = slot_place[:, :, None] == jnp.arange(slot_count, dtype=jnp.int32)[None, None, :]
    select = jnp.sum(slot_hot.astype(jnp.bfloat16), axis=1)
    weigh = jnp.sum(jnp.where(slot_hot, gate_weights[:, :, None], 0.0), axis=1)
    slot_gate = jnp.sum(weigh, axis=0)

    send_x = jnp.einsum("ts,td->sd", select, tokens, preferred_element_type=jnp.float32).astype(
        jnp.bfloat16
    )
    send_dy = jnp.einsum("ts,td->sd", select, cotangent, preferred_element_type=jnp.float32)
    send_c = (send_dy * slot_gate[:, None]).astype(jnp.bfloat16)
    arrived = exchange(jnp.concatenate([send_x, send_c], axis=1), expert_count, capacity)
    rows_x = arrived[:, :model_width]
    rows_c = arrived[:, model_width:]

    pre = jnp.dot(rows_x, weight_in, preferred_element_type=jnp.float32)
    gate_pre = pre[:, :hidden_units]
    up_pre = pre[:, hidden_units:]
    sigmoid_gate = jax.nn.sigmoid(gate_pre)
    activated = gate_pre * sigmoid_gate
    hidden = (activated * up_pre).astype(jnp.bfloat16)
    expert_out = jnp.dot(hidden, weight_out, preferred_element_type=jnp.float32).astype(
        jnp.bfloat16
    )
    returned = exchange(expert_out, expert_count, capacity)

    hidden_grad = jnp.einsum("sd,fd->sf", rows_c, weight_out, preferred_element_type=jnp.float32)
    slope = sigmoid_gate * (1.0 + gate_pre * (1.0 - sigmoid_gate))
    gate_up_grad = jnp.concatenate(
        [hidden_grad * up_pre * slope, hidden_grad * activated], axis=1
    ).astype(jnp.bfloat16)
    pick_grad = jnp.einsum(
        "sf,df->sd", gate_up_grad, weight_in, preferred_element_type=jnp.float32
    ).astype(jnp.bfloat16)
    in_cols = gate_up_grad.shape[1]
    rest = model_width - in_cols
    in_rows = model_width // group_count
    out_rows = hidden_units // group_count
    rest_rows = out_rows // (in_cols // rest)
    scale = 1.0 / group_count
    part_out = (
        jnp.einsum("sf,sd->fd", hidden, rows_c, preferred_element_type=jnp.float32) * scale
    ).astype(jnp.bfloat16).reshape(group_count, out_rows, model_width)
    part_in = (
        jnp.einsum("sd,sf->df", rows_x, gate_up_grad, preferred_element_type=jnp.float32) * scale
    ).astype(jnp.bfloat16).reshape(group_count, in_rows, in_cols)
    tail = part_out[:, :, in_cols:]
    bands = [tail[:, k * rest_rows : (k + 1) * rest_rows] for k in range(in_cols // rest)]
    joined = jnp.concatenate(
        [part_in, part_out[:, :, :in_cols], jnp.concatenate(bands, axis=2)], axis=1
    ).reshape(group_count * (in_rows + out_rows + rest_rows), in_cols)
    reduced = lax.psum_scatter(joined, "dp", scatter_dimension=0, tiled=True)
    back_grad = exchange(pick_grad, expert_count, capacity)

    mixed = jnp.dot(
        weigh,
        returned.astype(jnp.float32),
        precision=lax.Precision.HIGHEST,
        preferred_element_type=jnp.float32,
    ).astype(jnp.bfloat16)
    scores = jnp.einsum("td,sd->ts", cotangent, returned, preferred_element_type=jnp.float32)
    gate_grad = jnp.sum(jnp.where(slot_hot, scores[:, None, :], 0.0), axis=2)
    x_grad = jnp.einsum("ts,sd->td", select, back_grad, preferred_element_type=jnp.float32).astype(
        jnp.bfloat16
    )

    mixed, x_grad, gate_grad, reduced = lax.optimization_barrier((mixed, x_grad, gate_grad, reduced))
    expert_count = lax.axis_size("expert")
    step = expert_count // 4
    back_route = [(i, (i - step) % expert_count) for i in range(expert_count)]
    split = reduced.shape[0] // 2
    direct = partner_2(reduced[:split], "expert", half_bit)
    relayed = lax.ppermute(lax.ppermute(reduced[split:], "expert", back_route), "expert", back_route)
    reduced = jnp.where(is_moved, jnp.concatenate([direct, relayed], axis=0), reduced)
    grad_in = reduced[:in_rows]
    tail = reduced[in_rows + out_rows :]
    grad_out = jnp.concatenate(
        [reduced[in_rows : in_rows + out_rows],
         jnp.concatenate([tail[:, k * rest : (k + 1) * rest] for k in range(in_cols // rest)], axis=0)],
        axis=1,
    )
    return (mixed, x_grad, gate_grad, grad_in[None], grad_out[None])


def solution(mesh):
    placed = (
        P(("expert", "dp"), None),
        P(("expert", "dp"), None),
        P(("expert", "dp"), None),
        P(("expert", "dp"), None),
        P(),
        P("expert", None, None),
        P("expert", None, None),
    )
    return jax.shard_map(
        shards,
        mesh=mesh,
        in_specs=placed,
        out_specs=(
            P(("expert", "dp"), None),
            P(("expert", "dp"), None),
            P(("expert", "dp"), None),
            P("expert", "dp", None),
            P("expert", "dp", None),
        ),
        check_vma=False,
    )
```

```python
import jax
import jax.numpy as jnp
from jax import lax
from jax.sharding import PartitionSpec as P


def partner_2(block, axis, apart):
    count = lax.axis_size(axis)
    route = []
    for low in range(count):
        high = low | 1 << apart
        if high != low and high < count:
            route += [(low, high), (high, low)]
    return lax.ppermute(block, axis, route)


def pair_groups(expert_count, group_count):
    half = group_count // 2
    groups = []
    for flip in range(2):
        for z in range(half):
            members = []
            for e in range(expert_count):
                x_lo = flip ^ ((e >> 1) & 1)
                members.append(e * group_count + x_lo * half + z)
            groups.append(members)
    return groups


def exchange(block, expert_count, capacity):
    group_count = lax.axis_size("dp")
    shaped = block.reshape(expert_count, capacity, block.shape[-1])
    arrived = lax.all_to_all(
        shaped,
        ("expert", "dp"),
        split_axis=0,
        concat_axis=0,
        tiled=True,
        axis_index_groups=pair_groups(expert_count, group_count),
    )
    return arrived.reshape(expert_count * capacity, block.shape[-1])


def shards(tokens, cotangent, expert_ids, gate_weights, placement, w_in, w_out):
    expert_count = lax.axis_size("expert")
    group_count = lax.axis_size("dp")
    own_index = lax.axis_index("expert")
    tok_rows = tokens.shape[0]
    model_width = tokens.shape[1]
    hidden_units = w_out.shape[1]
    pick_count = expert_ids.shape[1]
    capacity = tok_rows // 8
    slot_count = expert_count * capacity
    pick_rows = tok_rows * pick_count
    half_bit = expert_count.bit_length() - 2
    expert_lane = jnp.arange(expert_count, dtype=jnp.int32)
    partner = jnp.sum(jnp.where(expert_lane == own_index, placement, 0))
    is_moved = partner != own_index
    weight_in = w_in[0]
    weight_out = w_out[0]

    device_hot = (expert_ids.reshape(-1)[:, None] == expert_lane[None, :]).astype(jnp.bfloat16)
    row_lane = jnp.arange(pick_rows, dtype=jnp.int32)
    earlier = (row_lane[None, :] < row_lane[:, None]).astype(jnp.bfloat16)
    slot_rank = jnp.dot(earlier, device_hot, preferred_element_type=jnp.float32).astype(jnp.int32)
    hot = device_hot.astype(jnp.int32)
    slot_place = jnp.sum((slot_rank + expert_lane[None, :] * capacity) * hot, axis=1)
    is_live = jnp.sum(hot, axis=1) > 0
    slot_place = jnp.where(is_live, slot_place, -1).reshape(tok_rows, pick_count)
    slot_hot = slot_place[:, :, None] == jnp.arange(slot_count, dtype=jnp.int32)[None, None, :]
    select = jnp.sum(slot_hot.astype(jnp.bfloat16), axis=1)
    weigh = jnp.sum(jnp.where(slot_hot, gate_weights[:, :, None], 0.0), axis=1)
    slot_gate = jnp.sum(weigh, axis=0)

    send_x = jnp.einsum("ts,td->sd", select, tokens, preferred_element_type=jnp.float32).astype(
        jnp.bfloat16
    )
    send_dy = jnp.einsum("ts,td->sd", select, cotangent, preferred_element_type=jnp.float32)
    send_c = (send_dy * slot_gate[:, None]).astype(jnp.bfloat16)
    arrived = exchange(jnp.concatenate([send_x, send_c], axis=1), expert_count, capacity)
    rows_x = arrived[:, :model_width]
    rows_c = arrived[:, model_width:]

    pre = jnp.dot(rows_x, weight_in, preferred_element_type=jnp.float32)
    gate_pre = pre[:, :hidden_units]
    up_pre = pre[:, hidden_units:]
    sigmoid_gate = jax.nn.sigmoid(gate_pre)
    activated = gate_pre * sigmoid_gate
    hidden = (activated * up_pre).astype(jnp.bfloat16)
    expert_out = jnp.dot(hidden, weight_out, preferred_element_type=jnp.float32).astype(
        jnp.bfloat16
    )
    returned = exchange(expert_out, expert_count, capacity)

    hidden_grad = jnp.einsum("sd,fd->sf", rows_c, weight_out, preferred_element_type=jnp.float32)
    slope = sigmoid_gate * (1.0 + gate_pre * (1.0 - sigmoid_gate))
    gate_up_grad = jnp.concatenate(
        [hidden_grad * up_pre * slope, hidden_grad * activated], axis=1
    ).astype(jnp.bfloat16)
    pick_grad = jnp.einsum(
        "sf,df->sd", gate_up_grad, weight_in, preferred_element_type=jnp.float32
    ).astype(jnp.bfloat16)
    in_cols = gate_up_grad.shape[1]
    rest = model_width - in_cols
    in_rows = model_width // group_count
    out_rows = hidden_units // group_count
    rest_rows = out_rows // (in_cols // rest)
    scale = 1.0 / group_count
    part_out = (
        jnp.einsum("sf,sd->fd", hidden, rows_c[:, :in_cols], preferred_element_type=jnp.float32) * scale
    ).astype(jnp.bfloat16).reshape(group_count, out_rows, in_cols)
    part_in = (
        jnp.einsum("sd,sf->df", rows_x, gate_up_grad, preferred_element_type=jnp.float32) * scale
    ).astype(jnp.bfloat16).reshape(group_count, in_rows, in_cols)
    band_count = in_cols // rest
    hidden_bands = hidden.reshape(hidden.shape[0], group_count, band_count, rest_rows)
    bands = (
        jnp.einsum("sgkr,sd->grkd", hidden_bands, rows_c[:, in_cols:], preferred_element_type=jnp.float32)
        * scale
    ).astype(jnp.bfloat16).reshape(group_count, rest_rows, in_cols)
    joined = jnp.concatenate([part_in, part_out, bands], axis=1).reshape(
        group_count * (in_rows + out_rows + rest_rows), in_cols
    )
    reduced = lax.psum_scatter(joined, "dp", scatter_dimension=0, tiled=True)
    back_grad = exchange(pick_grad, expert_count, capacity)

    mixed = jnp.dot(
        weigh,
        returned.astype(jnp.float32),
        precision=lax.Precision.HIGHEST,
        preferred_element_type=jnp.float32,
    ).astype(jnp.bfloat16)
    scores = jnp.einsum("td,sd->ts", cotangent, returned, preferred_element_type=jnp.float32)
    gate_grad = jnp.sum(jnp.where(slot_hot, scores[:, None, :], 0.0), axis=2)
    x_grad = jnp.einsum("ts,sd->td", select, back_grad, preferred_element_type=jnp.float32).astype(
        jnp.bfloat16
    )

    mixed, x_grad, gate_grad, reduced = lax.optimization_barrier((mixed, x_grad, gate_grad, reduced))
    swapped = partner_2(reduced, "expert", half_bit)
    reduced = jnp.where(is_moved, swapped, reduced)
    grad_in = reduced[:in_rows]
    tail = reduced[in_rows + out_rows :]
    grad_out = jnp.concatenate(
        [reduced[in_rows : in_rows + out_rows],
         jnp.concatenate([tail[:, k * rest : (k + 1) * rest] for k in range(in_cols // rest)], axis=0)],
        axis=1,
    )
    return (mixed, x_grad, gate_grad, grad_in[None], grad_out[None])


def solution(mesh):
    placed = (
        P(("expert", "dp"), None),
        P(("expert", "dp"), None),
        P(("expert", "dp"), None),
        P(("expert", "dp"), None),
        P(),
        P("expert", None, None),
        P("expert", None, None),
    )
    return jax.shard_map(
        shards,
        mesh=mesh,
        in_specs=placed,
        out_specs=(
            P(("expert", "dp"), None),
            P(("expert", "dp"), None),
            P(("expert", "dp"), None),
            P("expert", "dp", None),
            P("expert", "dp", None),
        ),
        check_vma=False,
    )
```

```python
import jax
import jax.numpy as jnp
from jax import lax
from jax.sharding import PartitionSpec as P


def partner_2(block, axis, apart):
    count = lax.axis_size(axis)
    route = []
    for low in range(count):
        high = low | 1 << apart
        if high != low and high < count:
            route += [(low, high), (high, low)]
    return lax.ppermute(block, axis, route)


def pair_groups(expert_count, group_count):
    half = group_count // 2
    groups = []
    for flip in range(2):
        for z in range(half):
            members = []
            for e in range(expert_count):
                x_lo = flip ^ ((e >> 1) & 1)
                members.append(e * group_count + x_lo * half + z)
            groups.append(members)
    return groups


def exchange(block, expert_count, capacity):
    group_count = lax.axis_size("dp")
    shaped = block.reshape(expert_count, capacity, block.shape[-1])
    arrived = lax.all_to_all(
        shaped,
        ("expert", "dp"),
        split_axis=0,
        concat_axis=0,
        tiled=True,
        axis_index_groups=pair_groups(expert_count, group_count),
    )
    return arrived.reshape(expert_count * capacity, block.shape[-1])


def shards(tokens, cotangent, expert_ids, gate_weights, placement, w_in, w_out):
    expert_count = lax.axis_size("expert")
    group_count = lax.axis_size("dp")
    own_index = lax.axis_index("expert")
    tok_rows = tokens.shape[0]
    model_width = tokens.shape[1]
    hidden_units = w_out.shape[1]
    pick_count = expert_ids.shape[1]
    capacity = tok_rows // 8
    slot_count = expert_count * capacity
    pick_rows = tok_rows * pick_count
    half_bit = expert_count.bit_length() - 2
    expert_lane = jnp.arange(expert_count, dtype=jnp.int32)
    partner = jnp.sum(jnp.where(expert_lane == own_index, placement, 0))
    is_moved = partner != own_index
    weight_in = w_in[0]
    weight_out = w_out[0]

    device_hot = (expert_ids.reshape(-1)[:, None] == expert_lane[None, :]).astype(jnp.bfloat16)
    row_lane = jnp.arange(pick_rows, dtype=jnp.int32)
    earlier = (row_lane[None, :] < row_lane[:, None]).astype(jnp.bfloat16)
    slot_rank = jnp.dot(earlier, device_hot, preferred_element_type=jnp.float32).astype(jnp.int32)
    hot = device_hot.astype(jnp.int32)
    slot_place = jnp.sum((slot_rank + expert_lane[None, :] * capacity) * hot, axis=1)
    is_live = jnp.sum(hot, axis=1) > 0
    slot_place = jnp.where(is_live, slot_place, -1).reshape(tok_rows, pick_count)
    slot_hot = slot_place[:, :, None] == jnp.arange(slot_count, dtype=jnp.int32)[None, None, :]
    select = jnp.sum(slot_hot.astype(jnp.bfloat16), axis=1)
    weigh = jnp.sum(jnp.where(slot_hot, gate_weights[:, :, None], 0.0), axis=1)
    slot_gate = jnp.sum(weigh, axis=0)

    send_x = jnp.einsum("ts,td->sd", select, tokens, preferred_element_type=jnp.float32).astype(
        jnp.bfloat16
    )
    send_dy = jnp.einsum("ts,td->sd", select, cotangent, preferred_element_type=jnp.float32)
    send_c = (send_dy * slot_gate[:, None]).astype(jnp.bfloat16)
    arrived = exchange(jnp.concatenate([send_x, send_c], axis=1), expert_count, capacity)
    rows_x = arrived[:, :model_width]
    rows_c = arrived[:, model_width:]

    pre = jnp.dot(rows_x, weight_in, preferred_element_type=jnp.float32)
    gate_pre = pre[:, :hidden_units]
    up_pre = pre[:, hidden_units:]
    sigmoid_gate = jax.nn.sigmoid(gate_pre)
    activated = gate_pre * sigmoid_gate
    hidden = (activated * up_pre).astype(jnp.bfloat16)
    expert_out = jnp.dot(hidden, weight_out, preferred_element_type=jnp.float32).astype(
        jnp.bfloat16
    )
    returned = exchange(expert_out, expert_count, capacity)

    hidden_grad = jnp.einsum("sd,fd->sf", rows_c, weight_out, preferred_element_type=jnp.float32)
    slope = sigmoid_gate * (1.0 + gate_pre * (1.0 - sigmoid_gate))
    gate_up_grad = jnp.concatenate(
        [hidden_grad * up_pre * slope, hidden_grad * activated], axis=1
    ).astype(jnp.bfloat16)
    pick_grad = jnp.einsum(
        "sf,df->sd", gate_up_grad, weight_in, preferred_element_type=jnp.float32
    ).astype(jnp.bfloat16)
    in_cols = gate_up_grad.shape[1]
    rest = model_width - in_cols
    in_rows = model_width // group_count
    out_rows = hidden_units // group_count
    rest_rows = out_rows // (in_cols // rest)
    scale = 1.0 / group_count
    part_out = (
        jnp.einsum("sf,sd->fd", hidden, rows_c[:, :in_cols], preferred_element_type=jnp.float32) * scale
    ).astype(jnp.bfloat16).reshape(group_count, out_rows, in_cols)
    part_in = (
        jnp.einsum("sd,sf->df", rows_x, gate_up_grad, preferred_element_type=jnp.float32) * scale
    ).astype(jnp.bfloat16).reshape(group_count, in_rows, in_cols)
    band_count = in_cols // rest
    hidden_bands = hidden.reshape(hidden.shape[0], group_count, band_count, rest_rows)
    bands = (
        jnp.einsum("sgkr,sd->grkd", hidden_bands, rows_c[:, in_cols:], preferred_element_type=jnp.float32)
        * scale
    ).astype(jnp.bfloat16).reshape(group_count, rest_rows, in_cols)
    joined = jnp.concatenate([part_in, part_out, bands], axis=1).reshape(
        group_count * (in_rows + out_rows + rest_rows), in_cols
    )
    reduced = lax.psum_scatter(joined, "dp", scatter_dimension=0, tiled=True)
    back_grad = exchange(pick_grad, expert_count, capacity)

    mixed = jnp.dot(
        weigh,
        returned.astype(jnp.float32),
        precision=lax.Precision.HIGHEST,
        preferred_element_type=jnp.float32,
    ).astype(jnp.bfloat16)
    scores = jnp.einsum("td,sd->ts", cotangent, returned, preferred_element_type=jnp.float32)
    gate_grad = jnp.sum(jnp.where(slot_hot, scores[:, None, :], 0.0), axis=2)
    x_grad = jnp.einsum("ts,sd->td", select, back_grad, preferred_element_type=jnp.float32).astype(
        jnp.bfloat16
    )

    mixed, x_grad, gate_grad, reduced = lax.optimization_barrier((mixed, x_grad, gate_grad, reduced))
    swapped = partner_2(reduced, "expert", half_bit)

    def unpack(block):
        tail = block[in_rows + out_rows :]
        bands_back = [tail[:, k * rest : (k + 1) * rest] for k in range(in_cols // rest)]
        out_block = jnp.concatenate(
            [block[in_rows : in_rows + out_rows], jnp.concatenate(bands_back, axis=0)], axis=1
        )
        return block[:in_rows], out_block

    in_moved, out_moved = unpack(swapped)
    in_kept, out_kept = unpack(reduced)
    grad_in = jnp.where(is_moved, in_moved, in_kept)
    grad_out = jnp.where(is_moved, out_moved, out_kept)
    return (mixed, x_grad, gate_grad, grad_in[None], grad_out[None])


def solution(mesh):
    placed = (
        P(("expert", "dp"), None),
        P(("expert", "dp"), None),
        P(("expert", "dp"), None),
        P(("expert", "dp"), None),
        P(),
        P("expert", None, None),
        P("expert", None, None),
    )
    return jax.shard_map(
        shards,
        mesh=mesh,
        in_specs=placed,
        out_specs=(
            P(("expert", "dp"), None),
            P(("expert", "dp"), None),
            P(("expert", "dp"), None),
            P("expert", "dp", None),
            P("expert", "dp", None),
        ),
        check_vma=False,
    )
```

```python
import jax
import jax.numpy as jnp
from jax import lax
from jax.sharding import PartitionSpec as P


def partner_2(block, axis, apart):
    count = lax.axis_size(axis)
    route = []
    for low in range(count):
        high = low | 1 << apart
        if high != low and high < count:
            route += [(low, high), (high, low)]
    return lax.ppermute(block, axis, route)


def pair_groups(expert_count, group_count):
    half = group_count // 2
    groups = []
    for flip in range(2):
        for z in range(half):
            members = []
            for e in range(expert_count):
                x_lo = flip ^ ((e >> 1) & 1)
                members.append(e * group_count + x_lo * half + z)
            groups.append(members)
    return groups


def exchange(block, expert_count, capacity):
    group_count = lax.axis_size("dp")
    shaped = block.reshape(expert_count, capacity, block.shape[-1])
    arrived = lax.all_to_all(
        shaped,
        ("expert", "dp"),
        split_axis=0,
        concat_axis=0,
        tiled=True,
        axis_index_groups=pair_groups(expert_count, group_count),
    )
    return arrived.reshape(expert_count * capacity, block.shape[-1])


def shards(tokens, cotangent, expert_ids, gate_weights, placement, w_in, w_out):
    expert_count = lax.axis_size("expert")
    group_count = lax.axis_size("dp")
    own_index = lax.axis_index("expert")
    tok_rows = tokens.shape[0]
    model_width = tokens.shape[1]
    hidden_units = w_out.shape[1]
    pick_count = expert_ids.shape[1]
    capacity = tok_rows // 8
    slot_count = expert_count * capacity
    pick_rows = tok_rows * pick_count
    half_bit = expert_count.bit_length() - 2
    expert_lane = jnp.arange(expert_count, dtype=jnp.int32)
    partner = jnp.sum(jnp.where(expert_lane == own_index, placement, 0))
    is_moved = partner != own_index
    weight_in = w_in[0]
    weight_out = w_out[0]

    device_hot = (expert_ids.reshape(-1)[:, None] == expert_lane[None, :]).astype(jnp.bfloat16)
    row_lane = jnp.arange(pick_rows, dtype=jnp.int32)
    earlier = (row_lane[None, :] < row_lane[:, None]).astype(jnp.bfloat16)
    slot_rank = jnp.dot(earlier, device_hot, preferred_element_type=jnp.float32).astype(jnp.int32)
    hot = device_hot.astype(jnp.int32)
    slot_place = jnp.sum((slot_rank + expert_lane[None, :] * capacity) * hot, axis=1)
    is_live = jnp.sum(hot, axis=1) > 0
    slot_place = jnp.where(is_live, slot_place, -1).reshape(tok_rows, pick_count)
    slot_hot = slot_place[:, :, None] == jnp.arange(slot_count, dtype=jnp.int32)[None, None, :]
    select = jnp.sum(slot_hot.astype(jnp.bfloat16), axis=1)
    weigh = jnp.sum(jnp.where(slot_hot, gate_weights[:, :, None], 0.0), axis=1)
    slot_gate = jnp.sum(weigh, axis=0)

    picked = jnp.einsum(
        "ts,td->sd", select, jnp.concatenate([tokens, cotangent], axis=1),
        preferred_element_type=jnp.float32,
    )
    column = jnp.arange(2 * model_width, dtype=jnp.int32)
    factor = jnp.where(column[None, :] < model_width, 1.0, slot_gate[:, None])
    arrived = exchange((picked * factor).astype(jnp.bfloat16), expert_count, capacity)
    rows_x = arrived[:, :model_width]
    rows_c = arrived[:, model_width:]

    pre = jnp.dot(rows_x, weight_in, preferred_element_type=jnp.float32)
    gate_pre = pre[:, :hidden_units]
    up_pre = pre[:, hidden_units:]
    sigmoid_gate = jax.nn.sigmoid(gate_pre)
    activated = gate_pre * sigmoid_gate
    hidden = (activated * up_pre).astype(jnp.bfloat16)
    expert_out = jnp.dot(hidden, weight_out, preferred_element_type=jnp.float32).astype(
        jnp.bfloat16
    )
    returned = exchange(expert_out, expert_count, capacity)

    hidden_grad = jnp.einsum("sd,fd->sf", rows_c, weight_out, preferred_element_type=jnp.float32)
    slope = sigmoid_gate * (1.0 + gate_pre * (1.0 - sigmoid_gate))
    gate_up_grad = jnp.concatenate(
        [hidden_grad * up_pre * slope, hidden_grad * activated], axis=1
    ).astype(jnp.bfloat16)
    pick_grad = jnp.einsum(
        "sf,df->sd", gate_up_grad, weight_in, preferred_element_type=jnp.float32
    ).astype(jnp.bfloat16)
    in_cols = gate_up_grad.shape[1]
    rest = model_width - in_cols
    in_rows = model_width // group_count
    out_rows = hidden_units // group_count
    rest_rows = out_rows // (in_cols // rest)
    scale = 1.0 / group_count
    part_out = (
        jnp.einsum("sf,sd->fd", hidden, rows_c[:, :in_cols], preferred_element_type=jnp.float32) * scale
    ).astype(jnp.bfloat16).reshape(group_count, out_rows, in_cols)
    part_in = (
        jnp.einsum("sd,sf->df", rows_x, gate_up_grad, preferred_element_type=jnp.float32) * scale
    ).astype(jnp.bfloat16).reshape(group_count, in_rows, in_cols)
    band_count = in_cols // rest
    hidden_bands = hidden.reshape(hidden.shape[0], group_count, band_count, rest_rows)
    bands = (
        jnp.einsum("sgkr,sd->grkd", hidden_bands, rows_c[:, in_cols:], preferred_element_type=jnp.float32)
        * scale
    ).astype(jnp.bfloat16).reshape(group_count, rest_rows, in_cols)
    joined = jnp.concatenate([part_in, part_out, bands], axis=1).reshape(
        group_count * (in_rows + out_rows + rest_rows), in_cols
    )
    reduced = lax.psum_scatter(joined, "dp", scatter_dimension=0, tiled=True)
    back_grad = exchange(pick_grad, expert_count, capacity)

    mixed = jnp.dot(
        weigh,
        returned.astype(jnp.float32),
        precision=lax.Precision.HIGHEST,
        preferred_element_type=jnp.float32,
    ).astype(jnp.bfloat16)
    scores = jnp.einsum("td,sd->ts", cotangent, returned, preferred_element_type=jnp.float32)
    gate_grad = jnp.sum(jnp.where(slot_hot, scores[:, None, :], 0.0), axis=2)
    x_grad = jnp.einsum("ts,sd->td", select, back_grad, preferred_element_type=jnp.float32).astype(
        jnp.bfloat16
    )

    mixed, x_grad, gate_grad, reduced = lax.optimization_barrier((mixed, x_grad, gate_grad, reduced))
    swapped = partner_2(reduced, "expert", half_bit)
    reduced = jnp.where(is_moved, swapped, reduced)
    grad_in = reduced[:in_rows]
    tail = reduced[in_rows + out_rows :]
    grad_out = jnp.concatenate(
        [reduced[in_rows : in_rows + out_rows],
         jnp.concatenate([tail[:, k * rest : (k + 1) * rest] for k in range(in_cols // rest)], axis=0)],
        axis=1,
    )
    return (mixed, x_grad, gate_grad, grad_in[None], grad_out[None])


def solution(mesh):
    placed = (
        P(("expert", "dp"), None),
        P(("expert", "dp"), None),
        P(("expert", "dp"), None),
        P(("expert", "dp"), None),
        P(),
        P("expert", None, None),
        P("expert", None, None),
    )
    return jax.shard_map(
        shards,
        mesh=mesh,
        in_specs=placed,
        out_specs=(
            P(("expert", "dp"), None),
            P(("expert", "dp"), None),
            P(("expert", "dp"), None),
            P("expert", "dp", None),
            P("expert", "dp", None),
        ),
        check_vma=False,
    )
```

```python
import jax
import jax.numpy as jnp
from jax import lax
from jax.sharding import PartitionSpec as P


def partner_2(block, axis, apart):
    count = lax.axis_size(axis)
    route = []
    for low in range(count):
        high = low | 1 << apart
        if high != low and high < count:
            route += [(low, high), (high, low)]
    return lax.ppermute(block, axis, route)


def pair_groups(expert_count, group_count):
    half = group_count // 2
    groups = []
    for flip in range(2):
        for z in range(half):
            members = []
            for e in range(expert_count):
                x_lo = flip ^ ((e >> 1) & 1)
                members.append(e * group_count + x_lo * half + z)
            groups.append(members)
    return groups


def exchange(block, expert_count, capacity):
    group_count = lax.axis_size("dp")
    shaped = block.reshape(expert_count, capacity, block.shape[-1])
    arrived = lax.all_to_all(
        shaped,
        ("expert", "dp"),
        split_axis=0,
        concat_axis=0,
        tiled=True,
        axis_index_groups=pair_groups(expert_count, group_count),
    )
    return arrived.reshape(expert_count * capacity, block.shape[-1])


def shards(tokens, cotangent, expert_ids, gate_weights, placement, w_in, w_out):
    expert_count = lax.axis_size("expert")
    group_count = lax.axis_size("dp")
    own_index = lax.axis_index("expert")
    tok_rows = tokens.shape[0]
    model_width = tokens.shape[1]
    hidden_units = w_out.shape[1]
    pick_count = expert_ids.shape[1]
    capacity = tok_rows // 8
    slot_count = expert_count * capacity
    pick_rows = tok_rows * pick_count
    half_bit = expert_count.bit_length() - 2
    expert_lane = jnp.arange(expert_count, dtype=jnp.int32)
    partner = jnp.sum(jnp.where(expert_lane == own_index, placement, 0))
    is_moved = partner != own_index
    weight_in = w_in[0]
    weight_out = w_out[0]

    device_hot = (expert_ids.reshape(-1)[:, None] == expert_lane[None, :]).astype(jnp.bfloat16)
    row_lane = jnp.arange(pick_rows, dtype=jnp.int32)
    earlier = (row_lane[None, :] < row_lane[:, None]).astype(jnp.bfloat16)
    slot_rank = jnp.dot(earlier, device_hot, preferred_element_type=jnp.float32).astype(jnp.int32)
    hot = device_hot.astype(jnp.int32)
    slot_place = jnp.sum((slot_rank + expert_lane[None, :] * capacity) * hot, axis=1)
    is_live = jnp.sum(hot, axis=1) > 0
    slot_place = jnp.where(is_live, slot_place, -1).reshape(tok_rows, pick_count)
    slot_hot = slot_place[:, :, None] == jnp.arange(slot_count, dtype=jnp.int32)[None, None, :]
    select = jnp.sum(slot_hot.astype(jnp.bfloat16), axis=1)
    weigh = jnp.sum(jnp.where(slot_hot, gate_weights[:, :, None], 0.0), axis=1)
    slot_gate = jnp.sum(weigh, axis=0)

    picked = jnp.einsum(
        "ts,td->sd", select, jnp.concatenate([tokens, cotangent], axis=1),
        preferred_element_type=jnp.float32,
    )
    column = jnp.arange(2 * model_width, dtype=jnp.int32)
    factor = jnp.where(column[None, :] < model_width, 1.0, slot_gate[:, None])
    arrived = exchange((picked * factor).astype(jnp.bfloat16), expert_count, capacity)
    rows_x = arrived[:, :model_width]
    rows_c = arrived[:, model_width:]

    pre = jnp.dot(rows_x, weight_in, preferred_element_type=jnp.float32)
    gate_pre = pre[:, :hidden_units]
    up_pre = pre[:, hidden_units:]
    sigmoid_gate = jax.nn.sigmoid(gate_pre)
    activated = gate_pre * sigmoid_gate
    hidden = (activated * up_pre).astype(jnp.bfloat16)
    expert_out = jnp.dot(hidden, weight_out, preferred_element_type=jnp.float32).astype(
        jnp.bfloat16
    )
    returned = exchange(expert_out, expert_count, capacity)

    hidden_grad = jnp.einsum("sd,fd->sf", rows_c, weight_out, preferred_element_type=jnp.float32)
    slope = sigmoid_gate * (1.0 + gate_pre * (1.0 - sigmoid_gate))
    gate_up_grad = jnp.concatenate(
        [hidden_grad * up_pre * slope, hidden_grad * activated], axis=1
    ).astype(jnp.bfloat16)
    pick_grad = jnp.einsum(
        "sf,df->sd", gate_up_grad, weight_in, preferred_element_type=jnp.float32
    ).astype(jnp.bfloat16)
    in_cols = gate_up_grad.shape[1]
    rest = model_width - in_cols
    in_rows = model_width // group_count
    out_rows = hidden_units // group_count
    rest_rows = out_rows // (in_cols // rest)
    scale = 1.0 / group_count
    part_out = (
        jnp.einsum("sf,sd->fd", hidden, rows_c[:, :in_cols], preferred_element_type=jnp.float32) * scale
    ).astype(jnp.bfloat16).reshape(group_count, out_rows, in_cols)
    part_in = (
        jnp.einsum("sd,sf->df", rows_x, gate_up_grad, preferred_element_type=jnp.float32) * scale
    ).astype(jnp.bfloat16).reshape(group_count, in_rows, in_cols)
    band_count = in_cols // rest
    hidden_bands = hidden.reshape(hidden.shape[0], group_count, band_count, rest_rows)
    bands = (
        jnp.einsum("sgkr,sd->grkd", hidden_bands, rows_c[:, in_cols:], preferred_element_type=jnp.float32)
        * scale
    ).astype(jnp.bfloat16).reshape(group_count, rest_rows, in_cols)
    joined = jnp.concatenate([part_in, part_out, bands], axis=1).reshape(
        group_count * (in_rows + out_rows + rest_rows), in_cols
    )
    reduced = lax.psum_scatter(joined, "dp", scatter_dimension=0, tiled=True)
    back_grad = exchange(pick_grad, expert_count, capacity)

    mixed = jnp.dot(
        weigh,
        returned.astype(jnp.float32),
        precision=lax.Precision.HIGHEST,
        preferred_element_type=jnp.float32,
    ).astype(jnp.bfloat16)
    scores = jnp.einsum("td,sd->ts", cotangent, returned, preferred_element_type=jnp.float32)
    gate_grad = jnp.sum(jnp.where(slot_hot, scores[:, None, :], 0.0), axis=2)
    x_grad = jnp.einsum("ts,sd->td", select, back_grad, preferred_element_type=jnp.float32).astype(
        jnp.bfloat16
    )

    swapped = partner_2(reduced, "expert", half_bit)
    reduced = jnp.where(is_moved, swapped, reduced)
    grad_in = reduced[:in_rows]
    tail = reduced[in_rows + out_rows :]
    grad_out = jnp.concatenate(
        [reduced[in_rows : in_rows + out_rows],
         jnp.concatenate([tail[:, k * rest : (k + 1) * rest] for k in range(in_cols // rest)], axis=0)],
        axis=1,
    )
    return (mixed, x_grad, gate_grad, grad_in[None], grad_out[None])


def solution(mesh):
    placed = (
        P(("expert", "dp"), None),
        P(("expert", "dp"), None),
        P(("expert", "dp"), None),
        P(("expert", "dp"), None),
        P(),
        P("expert", None, None),
        P("expert", None, None),
    )
    return jax.shard_map(
        shards,
        mesh=mesh,
        in_specs=placed,
        out_specs=(
            P(("expert", "dp"), None),
            P(("expert", "dp"), None),
            P(("expert", "dp"), None),
            P("expert", "dp", None),
            P("expert", "dp", None),
        ),
        check_vma=False,
    )
```
